32 devices in a mesh: group: 2 (over x), sector: 16 (over z, y, core).
Axes of the slice: x: 2, y: 2, z: 4, core: 2. Of those that a mesh axis runs over, the one named last changes fastest.
Arguments:
- wave: bfloat16 [32, 16, 256, 256], P(('group', 'sector')), parts along dimension 0, may hold values from -6 to 6
- left_ops: bfloat16 [384, 256, 256], P(('group', 'sector')), parts along dimension 0, may hold values from -0.375 to 0.375
- right_ops: bfloat16 [384, 256, 256], P(('group', 'sector')), parts along dimension 0, may hold values from -0.375 to 0.375
- deltas: int32 [384], P(('group', 'sector')), parts along dimension 0, may hold values from -1 to 1, as said below
- counts: int32 [32], P(('group', 'sector')), parts along dimension 0, may hold values from 2 to 12, as said below
Outputs:
- sigma: bfloat16 [32, 16, 256, 256], P(('group', 'sector')), parts along dimension 0
The draws below stay inside these ranges and needn't reach their ends.
There are 2 independent parts, one for each index of `group`. The reference program is written for one: setup_inputs(seed, part) draws one part's arguments, and reference() takes and returns one part's arrays. A program takes and returns all parts, laid end to end along the dimension named above; each array names one. Nothing has to cross between parts.
Inputs may be any that keep to these rules, and one draw needn't show every extreme that they name: `counts`: some sector has exactly 12 live slots in every draw; slots at or beyond a sector's count are unused. Every sector has 2 or more live slots. In each aligned pair of sectors 2i and 2i + 1 at most one has more than 6 live slots, and every other sector has 2 or 3 live slots. `deltas`: slot 0 of every sector reads the sector below it (offset -1) and slot 1 the sector above it (offset +1).
All inputs are finite; a program needn't handle non-finite values.
Results may differ from the reference program's by a relative error of at most 0.0049.
Values may be sent and summed in bfloat16 or wider, within the bound.
No kernel may reach another device: no remote copies, remote signals or barrier semaphores. Data moves between devices by JAX's collectives and lax.ppermute only.
A program may use at most 64 MiB of HBM per device.

```python
import jax
import jax.numpy as jnp
from jax import lax

M = 256
ROOTS = 16
SLOTS = 12
SECTORS = 16


def draw_deltas(key, part):
    random_part = jax.random.randint(jax.random.fold_in(key, 11), (SECTORS * SLOTS,), -1, 2)
    slot_ids = jnp.arange(SECTORS * SLOTS, dtype=jnp.int32) % SLOTS
    values = jnp.where(slot_ids == 0, -1, jnp.where(slot_ids == 1, 1, random_part))
    return values.astype(jnp.int32)


def draw_counts(key, part):
    first_key, second_key, third_key, fourth_key = jax.random.split(key, 4)
    pairs_total = SECTORS // 2
    lighter = jax.random.randint(first_key, (SECTORS,), 2, max(2, SLOTS // 4) + 1)
    loaded_pair = jax.random.randint(second_key, (pairs_total,), 0, 4) != 0
    forced = jax.random.randint(third_key, (), 0, pairs_total)
    loaded_pair = loaded_pair.at[forced].set(True)
    member = jax.random.randint(fourth_key, (pairs_total,), 0, 2)
    sector_ids = jnp.arange(SECTORS, dtype=jnp.int32)
    pair_of = sector_ids // 2
    heavy = jnp.logical_and(loaded_pair[pair_of], sector_ids % 2 == member[pair_of])
    values = jnp.where(heavy, SLOTS, lighter)
    return values.astype(jnp.int32)


def steps_of(key, extent, cuts, smallest, top_value):
    def one(position, blocks):
        draws = jax.random.uniform(jax.random.fold_in(jax.random.fold_in(key, 6), position), (blocks,), jnp.float32, smallest / len(cuts), top_value / len(cuts))
        return jnp.repeat(jnp.exp(draws), extent[position] // blocks).reshape((-1,) + (1,) * (len(extent) - position - 1))

    gain = one(*cuts[0])
    for cut in cuts[1:]:
        gain = gain * one(*cut)
    return gain


def gaussian(stream_key, extent, deviation, reach, shards=(), kind=jnp.bfloat16):
    values = deviation * jax.random.normal(stream_key, extent, jnp.float32)
    if shards:
        values = values * steps_of(stream_key, extent, shards, -0.22, 0.18)
    return jnp.clip(values, -reach, reach).astype(kind)


def setup_inputs(seed: int = 0, part: int = 0) -> dict:
    streams_of = jax.random.split(jax.random.key(seed), 6)
    part_keys = jax.random.split(jax.random.fold_in(streams_of[5], part), 6)
    wave = gaussian(part_keys[0], (SECTORS, ROOTS, M, M), 1.0, 6.0, ((0, 16),))
    left_ops = gaussian(part_keys[1], (SECTORS * SLOTS, M, M), M ** -0.5, 0.375, ((0, 16),))
    right_ops = gaussian(part_keys[2], (SECTORS * SLOTS, M, M), M ** -0.5, 0.375, ((0, 16),))
    deltas = draw_deltas(jax.random.fold_in(jax.random.fold_in(streams_of[5], part), 71), part)
    counts = draw_counts(jax.random.fold_in(jax.random.fold_in(streams_of[5], part), 71), part)
    return {"wave": wave, "left_ops": left_ops, "right_ops": right_ops, "deltas": deltas, "counts": counts}


def reference(wave, left_ops, right_ops, deltas, counts):
    border = jnp.zeros((1, ROOTS, M, M), jnp.bfloat16)
    padded = jnp.concatenate([border, wave, border], 0)

    def one_sector(sector):
        def add_pair(slot_index, running):
            pair = (sector * SLOTS + slot_index).astype(jnp.int32)
            source = (sector + 1 + deltas[pair]).astype(jnp.int32)
            source_block = lax.dynamic_index_in_dim(padded, source, 0, keepdims=False)
            left_op = lax.dynamic_index_in_dim(left_ops, pair, 0, keepdims=False)
            right_op = lax.dynamic_index_in_dim(right_ops, pair, 0, keepdims=False)
            mixed = jnp.einsum("ij,rjk->rik", left_op.astype(jnp.float32), source_block.astype(jnp.float32)).astype(jnp.bfloat16)
            return running + jnp.einsum("rik,lk->ril", mixed.astype(jnp.float32), right_op.astype(jnp.float32))

        running = lax.fori_loop(jnp.int32(0), counts[sector].astype(jnp.int32), add_pair, jnp.zeros((ROOTS, M, M), jnp.float32))
        return running.astype(jnp.bfloat16)

    return lax.map(one_sector, jnp.arange(SECTORS, dtype=jnp.int32))
```

```python
import functools

import jax
import jax.numpy as jnp
from jax import lax
from jax.experimental import pallas as pl
from jax.experimental.pallas import tpu as pltpu
from jax.sharding import PartitionSpec as P

CHUNKS = 4


def neighbours(block, axis):
    count = lax.axis_size(axis)
    from_prev = lax.ppermute(block, axis, [(i, i + 1) for i in range(count - 1)])
    from_next = lax.ppermute(block, axis, [(i + 1, i) for i in range(count - 1)])
    return from_prev, from_next


def pair_kernel(deltas_ref, count_ref, prev_ref, own_ref, next_ref, left_ref, right_ref, out_ref, acc_ref):
    k = pl.program_id(0)

    @pl.when(k == 0)
    def _():
        acc_ref[...] = jnp.zeros_like(acc_ref)

    @pl.when(k < count_ref[0])
    def _():
        delta = deltas_ref[k]
        left = left_ref[0]
        right = right_ref[0]

        def run(src_ref):
            def body(r, carry):
                mixed = jnp.dot(left, src_ref[r], preferred_element_type=jnp.float32).astype(jnp.bfloat16)
                acc_ref[r] += lax.dot_general(
                    mixed, right, (((1,), (1,)), ((), ())), preferred_element_type=jnp.float32
                )
                return carry

            lax.fori_loop(0, src_ref.shape[0], body, 0)

        for d, ref in ((-1, prev_ref), (0, own_ref), (1, next_ref)):
            pl.when(delta == d)(functools.partial(run, ref))

    @pl.when(k == pl.num_programs(0) - 1)
    def _():
        out_ref[...] = acc_ref[...].astype(out_ref.dtype)


def apply_pairs(prev, own, nxt, left_ops, right_ops, deltas, count):
    rows, width = own.shape[0], own.shape[1]
    slots = left_ops.shape[0]
    whole = pl.BlockSpec((rows, width, width), lambda k, d, c: (0, 0, 0))
    per_slot = pl.BlockSpec((1, width, width), lambda k, d, c: (jnp.minimum(k, c[0] - 1), 0, 0))
    flops = 4 * slots * rows * width ** 3
    moved = 2 * (3 * rows * width * width + 2 * slots * width * width + rows * width * width)
    return pl.pallas_call(
        pair_kernel,
        out_shape=jax.ShapeDtypeStruct((rows, width, width), jnp.bfloat16),
        grid_spec=pltpu.PrefetchScalarGridSpec(
            num_scalar_prefetch=2,
            grid=(slots,),
            in_specs=[whole, whole, whole, per_slot, per_slot],
            out_specs=whole,
            scratch_shapes=[pltpu.VMEM((rows, width, width), jnp.float32)],
        ),
        cost_estimate=pl.CostEstimate(flops=flops, bytes_accessed=moved, transcendentals=0),
    )(deltas, count, prev, own, nxt, left_ops, right_ops)


def on_device(wave, left_ops, right_ops, deltas, counts):
    own = wave[0]
    roots = own.shape[0]
    step = roots // CHUNKS
    outs = []
    for j in range(CHUNKS):
        part = own[j * step:(j + 1) * step]
        prev, nxt = neighbours(part, "sector")
        outs.append(apply_pairs(prev, part, nxt, left_ops, right_ops, deltas, counts))
    return jnp.concatenate(outs, 0)[None]


def solution(mesh):
    return jax.shard_map(
        on_device,
        mesh=mesh,
        in_specs=(
            P(("group", "sector"), None, None, None),
            P(("group", "sector"), None, None),
            P(("group", "sector"), None, None),
            P(("group", "sector")),
            P(("group", "sector")),
        ),
        out_specs=P(("group", "sector"), None, None, None),
        check_vma=False,
    )
```

```python
import functools

import jax
import jax.numpy as jnp
from jax import lax
from jax.experimental import pallas as pl
from jax.experimental.pallas import tpu as pltpu
from jax.sharding import PartitionSpec as P

CHUNKS = 4


def neighbours(block, axis):
    count = lax.axis_size(axis)
    from_prev = lax.ppermute(block, axis, [(i, i + 1) for i in range(count - 1)])
    from_next = lax.ppermute(block, axis, [(i + 1, i) for i in range(count - 1)])
    return from_prev, from_next


def pair_kernel(deltas_ref, count_ref, prev_ref, own_ref, next_ref, left_ref, right_ref, out_ref, acc_ref, mixed_ref):
    k = pl.program_id(0)
    rows, width = own_ref.shape[0], own_ref.shape[1]

    @pl.when(k == 0)
    def _():
        acc_ref[...] = jnp.zeros_like(acc_ref)

    @pl.when(k < count_ref[0])
    def _():
        delta = deltas_ref[k]
        left = left_ref[0]

        def run(src_ref):
            for r in range(rows):
                mixed_ref[pl.ds(r * width, width), :] = jnp.dot(
                    left, src_ref[r], preferred_element_type=jnp.float32
                ).astype(jnp.bfloat16)

        for d, ref in ((-1, prev_ref), (0, own_ref), (1, next_ref)):
            pl.when(delta == d)(functools.partial(run, ref))
        acc_ref[...] += lax.dot_general(
            mixed_ref[...], right_ref[0], (((1,), (1,)), ((), ())), preferred_element_type=jnp.float32
        )

    @pl.when(k == pl.num_programs(0) - 1)
    def _():
        for r in range(rows):
            out_ref[r] = acc_ref[pl.ds(r * width, width), :].astype(out_ref.dtype)


def apply_pairs(prev, own, nxt, left_ops, right_ops, deltas, count):
    rows, width = own.shape[0], own.shape[1]
    slots = left_ops.shape[0]
    whole = pl.BlockSpec((rows, width, width), lambda k, d, c: (0, 0, 0))
    per_slot = pl.BlockSpec((1, width, width), lambda k, d, c: (jnp.minimum(k, c[0] - 1), 0, 0))
    flops = 4 * slots * rows * width ** 3
    moved = 2 * (3 * rows * width * width + 2 * slots * width * width + rows * width * width)
    return pl.pallas_call(
        pair_kernel,
        out_shape=jax.ShapeDtypeStruct((rows, width, width), jnp.bfloat16),
        grid_spec=pltpu.PrefetchScalarGridSpec(
            num_scalar_prefetch=2,
            grid=(slots,),
            in_specs=[whole, whole, whole, per_slot, per_slot],
            out_specs=whole,
            scratch_shapes=[
                pltpu.VMEM((rows * width, width), jnp.float32),
                pltpu.VMEM((rows * width, width), jnp.bfloat16),
            ],
        ),
        cost_estimate=pl.CostEstimate(flops=flops, bytes_accessed=moved, transcendentals=0),
    )(deltas, count, prev, own, nxt, left_ops, right_ops)


def on_device(wave, left_ops, right_ops, deltas, counts):
    own = wave[0]
    roots = own.shape[0]
    step = roots // CHUNKS
    outs = []
    for j in range(CHUNKS):
        part = own[j * step:(j + 1) * step]
        prev, nxt = neighbours(part, "sector")
        outs.append(apply_pairs(prev, part, nxt, left_ops, right_ops, deltas, counts))
    return jnp.concatenate(outs, 0)[None]


def solution(mesh):
    return jax.shard_map(
        on_device,
        mesh=mesh,
        in_specs=(
            P(("group", "sector"), None, None, None),
            P(("group", "sector"), None, None),
            P(("group", "sector"), None, None),
            P(("group", "sector")),
            P(("group", "sector")),
        ),
        out_specs=P(("group", "sector"), None, None, None),
        check_vma=False,
    )
```

```python
import functools

import jax
import jax.numpy as jnp
from jax import lax
from jax.experimental import pallas as pl
from jax.experimental.pallas import tpu as pltpu
from jax.sharding import PartitionSpec as P


def pair_kernel(deltas_ref, count_ref, table_ref, s0, s1, s2, s3, left_ref, right_ref, out_ref, acc_ref, mixed_ref):
    k = pl.program_id(0)
    rows, width = s0.shape[0], s0.shape[1]

    @pl.when(k == 0)
    def _():
        acc_ref[...] = jnp.zeros_like(acc_ref)

    @pl.when(k < count_ref[0])
    def _():
        which = table_ref[deltas_ref[k] + 1]
        left = left_ref[0]

        def run(src_ref):
            for r in range(rows):
                mixed_ref[pl.ds(r * width, width), :] = jnp.dot(
                    left, src_ref[r], preferred_element_type=jnp.float32
                ).astype(jnp.bfloat16)

        for m, ref in enumerate((s0, s1, s2, s3)):
            pl.when(which == m)(functools.partial(run, ref))
        acc_ref[...] += lax.dot_general(
            mixed_ref[...], right_ref[0], (((1,), (1,)), ((), ())), preferred_element_type=jnp.float32
        )

    @pl.when(k == pl.num_programs(0) - 1)
    def _():
        for r in range(rows):
            out_ref[r] = acc_ref[pl.ds(r * width, width), :].astype(out_ref.dtype)


def apply_pairs(sources, left_ops, right_ops, deltas, count, table):
    rows, width = sources[0].shape[0], sources[0].shape[1]
    slots = left_ops.shape[0]
    whole = pl.BlockSpec((rows, width, width), lambda k, d, c, t: (0, 0, 0))
    per_slot = pl.BlockSpec((1, width, width), lambda k, d, c, t: (jnp.minimum(k, c[0] - 1), 0, 0))
    flops = 4 * slots * rows * width ** 3
    moved = 2 * (4 * rows * width * width + 2 * slots * width * width + rows * width * width)
    return pl.pallas_call(
        pair_kernel,
        out_shape=jax.ShapeDtypeStruct((rows, width, width), jnp.bfloat16),
        grid_spec=pltpu.PrefetchScalarGridSpec(
            num_scalar_prefetch=3,
            grid=(slots,),
            in_specs=[whole] * 4 + [per_slot, per_slot],
            out_specs=whole,
            scratch_shapes=[
                pltpu.VMEM((rows * width, width), jnp.float32),
                pltpu.VMEM((rows * width, width), jnp.bfloat16),
            ],
        ),
        cost_estimate=pl.CostEstimate(flops=flops, bytes_accessed=moved, transcendentals=0),
    )(deltas, count, table, *sources, left_ops, right_ops)


def on_device(wave, left_ops, right_ops, deltas, counts):
    n = lax.axis_size("sector")
    me = lax.axis_index("sector")
    parity = me % 2
    own = wave[0]
    half = own.shape[0] // 2
    mine = lax.dynamic_slice_in_dim(own, parity * half, half, 0)
    other = lax.dynamic_slice_in_dim(own, (1 - parity) * half, half, 0)

    odd, even = range(1, n, 2), range(0, n, 2)
    near = [(j, j + 1) for j in odd if j + 1 < n] + [(j, j - 1) for j in even if j >= 2]
    far = [(j, j + 2) for j in odd if j + 2 < n] + [(j, j - 2) for j in even if j >= 2]
    partner = [(j, j ^ 1) for j in range(n)]

    from_near = lax.ppermute(other, "sector", near)
    from_far = lax.ppermute(mine, "sector", far)
    from_partner = lax.ppermute(other, "sector", partner)
    sources = (mine, from_near, from_far, from_partner)

    left_p = lax.ppermute(left_ops, "sector", partner)
    right_p = lax.ppermute(right_ops, "sector", partner)
    deltas_p = lax.ppermute(deltas, "sector", partner)
    counts_p = lax.ppermute(counts, "sector", partner)

    key = 1 + parity
    steps = jnp.arange(3, dtype=jnp.int32)
    own_table = lax.bitwise_xor(steps + parity, key).astype(jnp.int32)
    partner_table = lax.bitwise_xor(steps + 1 - parity, key).astype(jnp.int32)

    own_half = apply_pairs(sources, left_ops, right_ops, deltas, counts, own_table)
    partner_half = apply_pairs(sources, left_p, right_p, deltas_p, counts_p, partner_table)
    returned = lax.ppermute(partner_half, "sector", partner)

    out = jnp.zeros_like(own)
    out = lax.dynamic_update_slice_in_dim(out, own_half, parity * half, 0)
    out = lax.dynamic_update_slice_in_dim(out, returned, (1 - parity) * half, 0)
    return out[None]


def solution(mesh):
    return jax.shard_map(
        on_device,
        mesh=mesh,
        in_specs=(
            P(("group", "sector"), None, None, None),
            P(("group", "sector"), None, None),
            P(("group", "sector"), None, None),
            P(("group", "sector")),
            P(("group", "sector")),
        ),
        out_specs=P(("group", "sector"), None, None, None),
        check_vma=False,
    )
```

```python
import functools

import jax
import jax.numpy as jnp
from jax import lax
from jax.experimental import pallas as pl
from jax.experimental.pallas import tpu as pltpu
from jax.sharding import PartitionSpec as P


def pair_kernel(deltas_ref, count_ref, table_ref, sa, sb, left_ref, right_ref, *rest):
    if len(rest) == 4:
        start_ref, out_ref, acc_ref, mixed_ref = rest
    else:
        start_ref = None
        out_ref, acc_ref, mixed_ref = rest
    k = pl.program_id(0)
    rows, width = sa.shape[0], sa.shape[1]

    @pl.when(k == 0)
    def _():
        if start_ref is None:
            acc_ref[...] = jnp.zeros_like(acc_ref)
        else:
            acc_ref[...] = start_ref[...]

    which = table_ref[jnp.clip(deltas_ref[k], -1, 1) + 1]

    @pl.when(jnp.logical_and(k < count_ref[0], which < 2))
    def _():
        left = left_ref[0]

        def run(src_ref):
            for r in range(rows):
                mixed_ref[pl.ds(r * width, width), :] = jnp.dot(
                    left, src_ref[r], preferred_element_type=jnp.float32
                ).astype(jnp.bfloat16)

        for m, ref in enumerate((sa, sb)):
            pl.when(which == m)(functools.partial(run, ref))
        acc_ref[...] += lax.dot_general(
            mixed_ref[...], right_ref[0], (((1,), (1,)), ((), ())), preferred_element_type=jnp.float32
        )

    @pl.when(k == pl.num_programs(0) - 1)
    def _():
        out_ref[...] = acc_ref[...].astype(out_ref.dtype)


def apply_pairs(sources, left_ops, right_ops, deltas, count, table, start=None):
    rows, width = sources[0].shape[0], sources[0].shape[1]
    slots = left_ops.shape[0]
    whole = pl.BlockSpec((rows, width, width), lambda k, d, c, t: (0, 0, 0))
    flat = pl.BlockSpec((rows * width, width), lambda k, d, c, t: (0, 0))
    per_slot = pl.BlockSpec((1, width, width), lambda k, d, c, t: (jnp.minimum(k, c[0] - 1), 0, 0))
    flops = 4 * slots * rows * width ** 3 // 2
    moved = 2 * (2 * rows * width * width + 2 * slots * width * width) + 6 * rows * width * width
    extra = () if start is None else (start,)
    dtype = jnp.float32 if start is None else jnp.bfloat16
    return pl.pallas_call(
        pair_kernel,
        out_shape=jax.ShapeDtypeStruct((rows * width, width), dtype),
        grid_spec=pltpu.PrefetchScalarGridSpec(
            num_scalar_prefetch=3,
            grid=(slots,),
            in_specs=[whole] * 2 + [per_slot, per_slot] + [flat] * len(extra),
            out_specs=flat,
            scratch_shapes=[
                pltpu.VMEM((rows * width, width), jnp.float32),
                pltpu.VMEM((rows * width, width), jnp.bfloat16),
            ],
        ),
        cost_estimate=pl.CostEstimate(flops=flops, bytes_accessed=moved, transcendentals=0),
    )(deltas, count, table, *sources, left_ops, right_ops, *extra)


def on_device(wave, left_ops, right_ops, deltas, counts):
    n = lax.axis_size("sector")
    me = lax.axis_index("sector")
    parity = me % 2
    own = wave[0]
    half = own.shape[0] // 2
    mine = lax.dynamic_slice_in_dim(own, parity * half, half, 0)
    other = lax.dynamic_slice_in_dim(own, (1 - parity) * half, half, 0)

    odd, even = range(1, n, 2), range(0, n, 2)
    near = [(j, j + 1) for j in odd if j + 1 < n] + [(j, j - 1) for j in even if j >= 2]
    far = [(j, j + 2) for j in odd if j + 2 < n] + [(j, j - 2) for j in even if j >= 2]
    partner = [(j, j ^ 1) for j in range(n)]

    from_near = lax.ppermute(other, "sector", near)
    from_far = lax.ppermute(mine, "sector", far)
    from_partner = lax.ppermute(other, "sector", partner)
    sources = (mine, from_near, from_far, from_partner)

    left_p = lax.ppermute(left_ops, "sector", partner)
    right_p = lax.ppermute(right_ops, "sector", partner)
    deltas_p = lax.ppermute(deltas, "sector", partner)
    counts_p = lax.ppermute(counts, "sector", partner)

    key = 1 + parity
    steps = jnp.arange(3, dtype=jnp.int32)
    own_ids = lax.bitwise_xor(steps + parity, key)
    partner_ids = lax.bitwise_xor(steps + 1 - parity, key)
    on_chip = jnp.array([0, 2, 2, 1], jnp.int32)
    off_chip = jnp.array([2, 0, 1, 2], jnp.int32)
    local = (mine, from_partner)
    halos = (from_near, from_far)
    shape = own.shape[1:]

    partner_sum = apply_pairs(local, left_p, right_p, deltas_p, counts_p, on_chip[partner_ids])
    own_sum = apply_pairs(local, left_ops, right_ops, deltas, counts, on_chip[own_ids])
    own_sum, partner_sum, from_near, from_far = lax.optimization_barrier(
        (own_sum, partner_sum, from_near, from_far)
    )
    halos = (from_near, from_far)
    partner_half = apply_pairs(halos, left_p, right_p, deltas_p, counts_p, off_chip[partner_ids], partner_sum)
    partner_half = partner_half.reshape((half,) + shape)
    own_half = apply_pairs(halos, left_ops, right_ops, deltas, counts, off_chip[own_ids], own_sum)
    own_half = own_half.reshape((half,) + shape)
    returned = lax.ppermute(partner_half, "sector", partner)

    out = jnp.zeros_like(own)
    out = lax.dynamic_update_slice_in_dim(out, own_half, parity * half, 0)
    out = lax.dynamic_update_slice_in_dim(out, returned, (1 - parity) * half, 0)
    return out[None]


def solution(mesh):
    return jax.shard_map(
        on_device,
        mesh=mesh,
        in_specs=(
            P(("group", "sector"), None, None, None),
            P(("group", "sector"), None, None),
            P(("group", "sector"), None, None),
            P(("group", "sector")),
            P(("group", "sector")),
        ),
        out_specs=P(("group", "sector"), None, None, None),
        check_vma=False,
    )
```

```python
import functools

import jax
import jax.numpy as jnp
from jax import lax
from jax.experimental import pallas as pl
from jax.experimental.pallas import tpu as pltpu
from jax.sharding import PartitionSpec as P


def source_of(delta, parity, mine_first, second):
    pos = jnp.clip(delta, -1, 1) + 1 + (parity if mine_first else 1 - parity)
    phys = jnp.where(parity == 0, pos + 1 - 2 * (pos % 2), (pos + 2) % 4)
    if second:
        return jnp.where(phys == 1, 0, jnp.where(phys == 2, 1, 2))
    return jnp.where(phys == 0, 0, jnp.where(phys == 3, 1, 2))


def pair_kernel(mine_first, second, deltas_ref, count_ref, sa, sb, left_ref, right_ref, *rest):
    if second:
        start_ref, out_ref, acc_ref, mixed_ref = rest
        acc_ref[...] = start_ref[...]
    else:
        out_ref, acc_ref, mixed_ref = rest
        acc_ref[...] = jnp.zeros_like(acc_ref)
    rows, width = sa.shape[0], sa.shape[1]
    parity = lax.axis_index("sector") % 2

    def step(k, carry):
        which = source_of(deltas_ref[k], parity, mine_first, second)

        @pl.when(which < 2)
        def _():
            left = left_ref[k]

            def run(src_ref):
                for r in range(rows):
                    mixed_ref[pl.ds(r * width, width), :] = jnp.dot(
                        left, src_ref[r], preferred_element_type=jnp.float32
                    ).astype(jnp.bfloat16)

            for m, ref in enumerate((sa, sb)):
                pl.when(which == m)(functools.partial(run, ref))
            acc_ref[...] += lax.dot_general(
                mixed_ref[...], right_ref[k], (((1,), (1,)), ((), ())), preferred_element_type=jnp.float32
            )

        return carry

    lax.fori_loop(0, jnp.minimum(count_ref[0], left_ref.shape[0]), step, 0)
    out_ref[...] = acc_ref[...].astype(out_ref.dtype)


def apply_pairs(sources, left_ops, right_ops, deltas, count, mine_first, start=None):
    rows, width = sources[0].shape[0], sources[0].shape[1]
    slots = left_ops.shape[0]
    second = start is not None
    vmem = pl.BlockSpec(memory_space=pltpu.VMEM)
    smem = pl.BlockSpec(memory_space=pltpu.SMEM)
    flops = 4 * slots * rows * width ** 3 // 2
    moved = 2 * (2 * rows * width * width + 2 * slots * width * width) + 6 * rows * width * width
    extra = (start,) if second else ()
    return pl.pallas_call(
        functools.partial(pair_kernel, mine_first, second),
        out_shape=jax.ShapeDtypeStruct((rows * width, width), jnp.bfloat16 if second else jnp.float32),
        in_specs=[smem, smem] + [vmem] * (4 + len(extra)),
        out_specs=vmem,
        scratch_shapes=[
            pltpu.VMEM((rows * width, width), jnp.float32),
            pltpu.VMEM((rows * width, width), jnp.bfloat16),
        ],
        cost_estimate=pl.CostEstimate(flops=flops, bytes_accessed=moved, transcendentals=0),
    )(deltas, count, *sources, left_ops, right_ops, *extra)


def on_device(wave, left_ops, right_ops, deltas, counts):
    n = lax.axis_size("sector")
    me = lax.axis_index("sector")
    parity = me % 2
    own = wave[0]
    half = own.shape[0] // 2
    mine = lax.dynamic_slice_in_dim(own, parity * half, half, 0)
    other = lax.dynamic_slice_in_dim(own, (1 - parity) * half, half, 0)

    odd, even = range(1, n, 2), range(0, n, 2)
    near = [(j, j + 1) for j in odd if j + 1 < n] + [(j, j - 1) for j in even if j >= 2]
    far = [(j, j + 2) for j in odd if j + 2 < n] + [(j, j - 2) for j in even if j >= 2]
    partner = [(j, j ^ 1) for j in range(n)]

    from_near = lax.ppermute(other, "sector", near)
    from_far = lax.ppermute(mine, "sector", far)
    from_partner = lax.ppermute(other, "sector", partner)

    left_p = lax.ppermute(left_ops, "sector", partner)
    right_p = lax.ppermute(right_ops, "sector", partner)
    deltas_p = lax.ppermute(deltas, "sector", partner)
    counts_p = lax.ppermute(counts, "sector", partner)

    local = (mine, from_partner)
    shape = own.shape[1:]

    partner_sum = apply_pairs(local, left_p, right_p, deltas_p, counts_p, False)
    own_sum = apply_pairs(local, left_ops, right_ops, deltas, counts, True)
    own_sum, partner_sum, from_near, from_far = lax.optimization_barrier(
        (own_sum, partner_sum, from_near, from_far)
    )
    halos = (from_near, from_far)
    partner_half = apply_pairs(halos, left_p, right_p, deltas_p, counts_p, False, partner_sum)
    partner_half = partner_half.reshape((half,) + shape)
    own_half = apply_pairs(halos, left_ops, right_ops, deltas, counts, True, own_sum)
    own_half = own_half.reshape((half,) + shape)
    returned = lax.ppermute(partner_half, "sector", partner)

    out = jnp.zeros_like(own)
    out = lax.dynamic_update_slice_in_dim(out, own_half, parity * half, 0)
    out = lax.dynamic_update_slice_in_dim(out, returned, (1 - parity) * half, 0)
    return out[None]


def solution(mesh):
    return jax.shard_map(
        on_device,
        mesh=mesh,
        in_specs=(
            P(("group", "sector"), None, None, None),
            P(("group", "sector"), None, None),
            P(("group", "sector"), None, None),
            P(("group", "sector")),
            P(("group", "sector")),
        ),
        out_specs=P(("group", "sector"), None, None, None),
        check_vma=False,
    )
```

```python
import functools

import jax
import jax.numpy as jnp
from jax import lax
from jax.experimental import pallas as pl
from jax.experimental.pallas import tpu as pltpu
from jax.sharding import PartitionSpec as P


def source_of(delta, parity, mine_first, second):
    pos = jnp.clip(delta, -1, 1) + 1 + (parity if mine_first else 1 - parity)
    phys = jnp.where(parity == 0, pos + 1 - 2 * (pos % 2), (pos + 2) % 4)
    if second:
        return jnp.where(phys == 1, 0, jnp.where(phys == 2, 1, 2))
    return jnp.where(phys == 0, 0, jnp.where(phys == 3, 1, 2))


def pair_kernel(mine_first, second, deltas_ref, count_ref, sa, sb, left_ref, right_ref, *rest):
    if second:
        start_ref, out_ref, acc_ref, mixed_ref = rest
        acc_ref[...] = start_ref[...]
    else:
        out_ref, acc_ref, mixed_ref = rest
        acc_ref[...] = jnp.zeros_like(acc_ref)
    rows, width = sa.shape[0], sa.shape[1]
    parity = lax.axis_index("sector") % 2

    def step(k, carry):
        which = source_of(deltas_ref[k], parity, mine_first, second)

        @pl.when(which < 2)
        def _():
            left = left_ref[k]

            def run(src_ref):
                for r in range(rows):
                    mixed_ref[pl.ds(r * width, width), :] = jnp.dot(
                        left, src_ref[r], preferred_element_type=jnp.float32
                    ).astype(jnp.bfloat16)

            for m, ref in enumerate((sa, sb)):
                pl.when(which == m)(functools.partial(run, ref))
            acc_ref[...] += lax.dot_general(
                mixed_ref[...], right_ref[k], (((1,), (1,)), ((), ())), preferred_element_type=jnp.float32
            )

        return carry

    lax.fori_loop(0, jnp.minimum(count_ref[0], left_ref.shape[0]), step, 0)
    if mine_first and second:
        offset = pl.multiple_of(parity * (rows * width), rows * width)
        out_ref[pl.ds(offset, rows * width), :] = acc_ref[...].astype(out_ref.dtype)
    else:
        out_ref[...] = acc_ref[...].astype(out_ref.dtype)


def apply_pairs(sources, left_ops, right_ops, deltas, count, mine_first, start=None):
    rows, width = sources[0].shape[0], sources[0].shape[1]
    slots = left_ops.shape[0]
    second = start is not None
    vmem = pl.BlockSpec(memory_space=pltpu.VMEM)
    smem = pl.BlockSpec(memory_space=pltpu.SMEM)
    flops = 4 * slots * rows * width ** 3 // 2
    moved = 2 * (2 * rows * width * width + 2 * slots * width * width) + 6 * rows * width * width
    extra = (start,) if second else ()
    return pl.pallas_call(
        functools.partial(pair_kernel, mine_first, second),
        out_shape=jax.ShapeDtypeStruct(
            ((2 if mine_first and second else 1) * rows * width, width), jnp.bfloat16 if second else jnp.float32
        ),
        in_specs=[smem, smem] + [vmem] * (4 + len(extra)),
        out_specs=vmem,
        scratch_shapes=[
            pltpu.VMEM((rows * width, width), jnp.float32),
            pltpu.VMEM((rows * width, width), jnp.bfloat16),
        ],
        cost_estimate=pl.CostEstimate(flops=flops, bytes_accessed=moved, transcendentals=0),
    )(deltas, count, *sources, left_ops, right_ops, *extra)


def on_device(wave, left_ops, right_ops, deltas, counts):
    n = lax.axis_size("sector")
    me = lax.axis_index("sector")
    parity = me % 2
    own = wave[0]
    half = own.shape[0] // 2
    mine = lax.dynamic_slice_in_dim(own, parity * half, half, 0)
    other = lax.dynamic_slice_in_dim(own, (1 - parity) * half, half, 0)

    odd, even = range(1, n, 2), range(0, n, 2)
    near = [(j, j + 1) for j in odd if j + 1 < n] + [(j, j - 1) for j in even if j >= 2]
    far = [(j, j + 2) for j in odd if j + 2 < n] + [(j, j - 2) for j in even if j >= 2]
    partner = [(j, j ^ 1) for j in range(n)]

    from_near = lax.ppermute(other, "sector", near)
    from_far = lax.ppermute(mine, "sector", far)
    from_partner = lax.ppermute(other, "sector", partner)

    left_p = lax.ppermute(left_ops, "sector", partner)
    right_p = lax.ppermute(right_ops, "sector", partner)
    deltas_p = lax.ppermute(deltas, "sector", partner)
    counts_p = lax.ppermute(counts, "sector", partner)

    local = (mine, from_partner)
    shape = own.shape[1:]

    partner_sum = apply_pairs(local, left_p, right_p, deltas_p, counts_p, False)
    own_sum = apply_pairs(local, left_ops, right_ops, deltas, counts, True)
    own_sum, partner_sum, from_near, from_far = lax.optimization_barrier(
        (own_sum, partner_sum, from_near, from_far)
    )
    halos = (from_near, from_far)
    partner_half = apply_pairs(halos, left_p, right_p, deltas_p, counts_p, False, partner_sum)
    partner_half = partner_half.reshape((half,) + shape)
    out = apply_pairs(halos, left_ops, right_ops, deltas, counts, True, own_sum)
    out, partner_half = lax.optimization_barrier((out, partner_half))
    returned = lax.ppermute(partner_half, "sector", partner)
    out = lax.dynamic_update_slice_in_dim(out.reshape(own.shape), returned, (1 - parity) * half, 0)
    return out[None]


def solution(mesh):
    return jax.shard_map(
        on_device,
        mesh=mesh,
        in_specs=(
            P(("group", "sector"), None, None, None),
            P(("group", "sector"), None, None),
            P(("group", "sector"), None, None),
            P(("group", "sector")),
            P(("group", "sector")),
        ),
        out_specs=P(("group", "sector"), None, None, None),
        check_vma=False,
    )
```

```python
import functools

import jax
import jax.numpy as jnp
from jax import lax
from jax.experimental import pallas as pl
from jax.experimental.pallas import tpu as pltpu
from jax.sharding import PartitionSpec as P


def source_of(delta, parity, mine_first, second):
    pos = jnp.clip(delta, -1, 1) + 1 + (parity if mine_first else 1 - parity)
    phys = jnp.where(parity == 0, pos + 1 - 2 * (pos % 2), (pos + 2) % 4)
    if second:
        return jnp.where(phys == 1, 0, jnp.where(phys == 2, 1, 2))
    return jnp.where(phys == 0, 0, jnp.where(phys == 3, 1, 2))


def pair_kernel(mine_first, second, chunk, deltas_ref, count_ref, sa, sb, left_ref, right_ref, *rest):
    rows, width = sa.shape[0], sa.shape[1]
    size = rows * width
    parity = lax.axis_index("sector") % 2
    if second:
        start_ref, out_ref, acc_ref, mixed_ref = rest[0], rest[-3], rest[-2], rest[-1]
        acc_ref[...] = start_ref[pl.ds(chunk * size, size), :]
    else:
        out_ref, acc_ref, mixed_ref = rest
        acc_ref[...] = jnp.zeros_like(acc_ref)

    def step(k, carry):
        which = source_of(deltas_ref[k], parity, mine_first, second)

        @pl.when(which < 2)
        def _():
            left = left_ref[k]

            def run(src_ref):
                for r in range(rows):
                    mixed_ref[pl.ds(r * width, width), :] = jnp.dot(
                        left, src_ref[r], preferred_element_type=jnp.float32
                    ).astype(jnp.bfloat16)

            for m, ref in enumerate((sa, sb)):
                pl.when(which == m)(functools.partial(run, ref))
            acc_ref[...] += lax.dot_general(
                mixed_ref[...], right_ref[k], (((1,), (1,)), ((), ())), preferred_element_type=jnp.float32
            )

        return carry

    lax.fori_loop(0, jnp.minimum(count_ref[0], left_ref.shape[0]), step, 0)
    out_ref[...] = acc_ref[...].astype(out_ref.dtype)


def apply_pairs(sources, left_ops, right_ops, deltas, count, mine_first, start=None, chunk=0):
    rows, width = sources[0].shape[0], sources[0].shape[1]
    slots = left_ops.shape[0]
    second = start is not None
    vmem = pl.BlockSpec(memory_space=pltpu.VMEM)
    smem = pl.BlockSpec(memory_space=pltpu.SMEM)
    flops = 4 * slots * rows * width ** 3 // 2
    moved = 2 * (2 * rows * width * width + 2 * slots * width * width) + 6 * rows * width * width
    extra = (start,) if second else ()
    out_shape = jax.ShapeDtypeStruct((rows * width, width), jnp.bfloat16 if second else jnp.float32)
    return pl.pallas_call(
        functools.partial(pair_kernel, mine_first, second, chunk),
        out_shape=out_shape,
        in_specs=[smem, smem] + [vmem] * (4 + len(extra)),
        out_specs=vmem,
        scratch_shapes=[
            pltpu.VMEM((rows * width, width), jnp.float32),
            pltpu.VMEM((rows * width, width), jnp.bfloat16),
        ],
        cost_estimate=pl.CostEstimate(flops=flops, bytes_accessed=moved, transcendentals=0),
    )(deltas, count, *sources, left_ops, right_ops, *extra)


def on_device(wave, left_ops, right_ops, deltas, counts):
    n = lax.axis_size("sector")
    me = lax.axis_index("sector")
    parity = me % 2
    own = wave[0]
    half = own.shape[0] // 2
    mine = lax.dynamic_slice_in_dim(own, parity * half, half, 0)
    other = lax.dynamic_slice_in_dim(own, (1 - parity) * half, half, 0)

    odd, even = range(1, n, 2), range(0, n, 2)
    near = [(j, j + 1) for j in odd if j + 1 < n] + [(j, j - 1) for j in even if j >= 2]
    far = [(j, j + 2) for j in odd if j + 2 < n] + [(j, j - 2) for j in even if j >= 2]
    partner = [(j, j ^ 1) for j in range(n)]

    quarter = half // 2
    near_parts = [lax.ppermute(other[c * quarter:(c + 1) * quarter], "sector", near) for c in range(2)]
    far_parts = [lax.ppermute(mine[c * quarter:(c + 1) * quarter], "sector", far) for c in range(2)]
    from_partner = lax.ppermute(other, "sector", partner)

    left_p, right_p, deltas_p, counts_p = lax.ppermute((left_ops, right_ops, deltas, counts), "sector", partner)

    local = (mine, from_partner)
    shape = own.shape[1:]

    partner_sum = apply_pairs(local, left_p, right_p, deltas_p, counts_p, False)
    own_sum = apply_pairs(local, left_ops, right_ops, deltas, counts, True)
    own_sum, partner_sum, near_0, far_0 = lax.optimization_barrier(
        (own_sum, partner_sum, near_parts[0], far_parts[0])
    )
    partner_0 = apply_pairs((near_0, far_0), left_p, right_p, deltas_p, counts_p, False, partner_sum, 0)
    own_0 = apply_pairs((near_0, far_0), left_ops, right_ops, deltas, counts, True, own_sum, 0)
    partner_0, own_0, near_1, far_1 = lax.optimization_barrier((partner_0, own_0, near_parts[1], far_parts[1]))
    partner_1 = apply_pairs((near_1, far_1), left_p, right_p, deltas_p, counts_p, False, partner_sum, 1)
    own_1 = apply_pairs((near_1, far_1), left_ops, right_ops, deltas, counts, True, own_sum, 1)
    own_0, own_1, partner_0, partner_1 = lax.optimization_barrier((own_0, own_1, partner_0, partner_1))
    partner_half = jnp.concatenate([partner_0, partner_1], 0).reshape((half,) + shape)
    returned = lax.ppermute(partner_half, "sector", partner)
    out = jnp.zeros_like(own)
    out = lax.dynamic_update_slice_in_dim(out, own_0.reshape((quarter,) + shape), parity * half, 0)
    out = lax.dynamic_update_slice_in_dim(out, own_1.reshape((quarter,) + shape), parity * half + quarter, 0)
    out = lax.dynamic_update_slice_in_dim(out, returned, (1 - parity) * half, 0)
    return out[None]


def solution(mesh):
    return jax.shard_map(
        on_device,
        mesh=mesh,
        in_specs=(
            P(("group", "sector"), None, None, None),
            P(("group", "sector"), None, None),
            P(("group", "sector"), None, None),
            P(("group", "sector")),
            P(("group", "sector")),
        ),
        out_specs=P(("group", "sector"), None, None, None),
        check_vma=False,
    )
```

```python
import functools

import jax
import jax.numpy as jnp
from jax import lax
from jax.experimental import pallas as pl
from jax.experimental.pallas import tpu as pltpu
from jax.sharding import PartitionSpec as P


def source_of(delta, parity, mine_first, phase):
    pos = jnp.clip(delta, -1, 1) + 1 + (parity if mine_first else 1 - parity)
    phys = jnp.where(parity == 0, pos + 1 - 2 * (pos % 2), (pos + 2) % 4)
    if phase == 0:
        return jnp.where(phys == 0, 0, jnp.where(phys == 3, 1, 2))
    return jnp.where(phys == phase, 0, 2)


def pairs_kernel(phase, n_src, *refs):
    d_own, c_own, d_par, c_par = refs[:4]
    srcs = refs[4:4 + n_src]
    l_own, r_own, l_par, r_par = refs[4 + n_src:8 + n_src]
    rest = refs[8 + n_src:]
    if phase > 0:
        s_own, s_par = rest[:2]
        rest = rest[2:]
    else:
        s_own = s_par = None
    o_own, o_par, acc_ref, mixed_ref = rest
    rows, width = srcs[0].shape[0], srcs[0].shape[1]
    size = rows * width
    parity = lax.axis_index("sector") % 2
    jobs = (
        (False, d_par, c_par, l_par, r_par, s_par, o_par),
        (True, d_own, c_own, l_own, r_own, s_own, o_own),
    )
    for mine_first, deltas_ref, count_ref, left_ref, right_ref, start_ref, out_ref in jobs:
        if start_ref is None:
            acc_ref[...] = jnp.zeros_like(acc_ref)
        else:
            acc_ref[...] = start_ref[...]

        def step(k, carry, deltas_ref=deltas_ref, left_ref=left_ref, right_ref=right_ref, mine_first=mine_first):
            which = source_of(deltas_ref[k], parity, mine_first, phase)

            @pl.when(which < n_src)
            def _():
                left = left_ref[k]

                def run(src_ref):
                    for r in range(rows):
                        mixed_ref[pl.ds(r * width, width), :] = jnp.dot(
                            left, src_ref[r], preferred_element_type=jnp.float32
                        ).astype(jnp.bfloat16)

                for m, ref in enumerate(srcs):
                    pl.when(which == m)(functools.partial(run, ref))
                acc_ref[...] += lax.dot_general(
                    mixed_ref[...], right_ref[k], (((1,), (1,)), ((), ())), preferred_element_type=jnp.float32
                )

            return carry

        lax.fori_loop(0, jnp.minimum(count_ref[0], left_ref.shape[0]), step, 0)
        if phase == 2 and mine_first:
            offset = pl.multiple_of(parity * size, size)
            out_ref[pl.ds(offset, size), :] = acc_ref[...].astype(out_ref.dtype)
        else:
            out_ref[...] = acc_ref[...].astype(out_ref.dtype)


def apply_pairs(phase, sources, own_job, partner_job, starts=()):
    rows, width = sources[0].shape[0], sources[0].shape[1]
    size = rows * width
    left_ops, right_ops, deltas, counts = own_job
    left_p, right_p, deltas_p, counts_p = partner_job
    slots = left_ops.shape[0]
    vmem = pl.BlockSpec(memory_space=pltpu.VMEM)
    smem = pl.BlockSpec(memory_space=pltpu.SMEM)
    flops = 4 * slots * size * width * width // 2
    moved = 2 * (len(sources) * size * width + 4 * slots * width * width) + 16 * size * width
    if phase == 2:
        outs = (
            jax.ShapeDtypeStruct((2 * size, width), jnp.bfloat16),
            jax.ShapeDtypeStruct((size, width), jnp.bfloat16),
        )
    else:
        outs = (jax.ShapeDtypeStruct((size, width), jnp.float32),) * 2
    return pl.pallas_call(
        functools.partial(pairs_kernel, phase, len(sources)),
        out_shape=outs,
        in_specs=[smem] * 4 + [vmem] * (len(sources) + 4 + len(starts)),
        out_specs=(vmem, vmem),
        scratch_shapes=[
            pltpu.VMEM((size, width), jnp.float32),
            pltpu.VMEM((size, width), jnp.bfloat16),
        ],
        cost_estimate=pl.CostEstimate(flops=flops, bytes_accessed=moved, transcendentals=0),
    )(deltas, counts, deltas_p, counts_p, *sources, left_ops, right_ops, left_p, right_p, *starts)


def on_device(wave, left_ops, right_ops, deltas, counts):
    n = lax.axis_size("sector")
    me = lax.axis_index("sector")
    parity = me % 2
    own = wave[0]
    half = own.shape[0] // 2
    mine = lax.dynamic_slice_in_dim(own, parity * half, half, 0)
    other = lax.dynamic_slice_in_dim(own, (1 - parity) * half, half, 0)

    odd, even = range(1, n, 2), range(0, n, 2)
    near = [(j, j + 1) for j in odd if j + 1 < n] + [(j, j - 1) for j in even if j >= 2]
    far = [(j, j + 2) for j in odd if j + 2 < n] + [(j, j - 2) for j in even if j >= 2]
    partner = [(j, j ^ 1) for j in range(n)]

    from_near = lax.ppermute(other, "sector", near)
    from_far = lax.ppermute(mine, "sector", far)
    from_partner = lax.ppermute(other, "sector", partner)

    left_p = lax.ppermute(left_ops, "sector", partner)
    right_p = lax.ppermute(right_ops, "sector", partner)
    deltas_p = lax.ppermute(deltas, "sector", partner)
    counts_p = lax.ppermute(counts, "sector", partner)
    own_job = (left_ops, right_ops, deltas, counts)
    partner_job = (left_p, right_p, deltas_p, counts_p)

    own_sum, partner_sum = apply_pairs(0, (mine, from_partner), own_job, partner_job)
    own_sum, partner_sum, from_near = lax.optimization_barrier((own_sum, partner_sum, from_near))
    own_sum, partner_sum = apply_pairs(1, (from_near,), own_job, partner_job, (own_sum, partner_sum))
    own_sum, partner_sum, from_far = lax.optimization_barrier((own_sum, partner_sum, from_far))
    out, partner_half = apply_pairs(2, (from_far,), own_job, partner_job, (own_sum, partner_sum))

    returned = lax.ppermute(partner_half.reshape((half,) + own.shape[1:]), "sector", partner)
    out = lax.dynamic_update_slice_in_dim(out.reshape(own.shape), returned, (1 - parity) * half, 0)
    return out[None]


def solution(mesh):
    return jax.shard_map(
        on_device,
        mesh=mesh,
        in_specs=(
            P(("group", "sector"), None, None, None),
            P(("group", "sector"), None, None),
            P(("group", "sector"), None, None),
            P(("group", "sector")),
            P(("group", "sector")),
        ),
        out_specs=P(("group", "sector"), None, None, None),
        check_vma=False,
    )
```

```python
import functools

import jax
import jax.numpy as jnp
from jax import lax
from jax.experimental import pallas as pl
from jax.experimental.pallas import tpu as pltpu
from jax.sharding import PartitionSpec as P


def source_of(delta, parity, mine_first, phase):
    pos = jnp.clip(delta, -1, 1) + 1 + (parity if mine_first else 1 - parity)
    phys = jnp.where(parity == 0, pos + 1 - 2 * (pos % 2), (pos + 2) % 4)
    if phase == 0:
        return jnp.where(phys == 0, 0, jnp.where(phys == 3, 1, 2))
    return jnp.where(phys == phase, 0, 2)


def pairs_kernel(phase, n_src, *refs):
    d_own, c_own, d_par, c_par = refs[:4]
    srcs = refs[4:4 + n_src]
    l_own, r_own, l_par, r_par = refs[4 + n_src:8 + n_src]
    rest = refs[8 + n_src:]
    if phase > 0:
        s_own, s_par = rest[:2]
        rest = rest[2:]
    else:
        s_own = s_par = None
    o_own, o_par, acc_ref, mixed_ref = rest
    rows, width = srcs[0].shape[0], srcs[0].shape[1]
    size = rows * width
    parity = lax.axis_index("sector") % 2
    jobs = (
        (False, d_par, c_par, l_par, r_par, s_par, o_par),
        (True, d_own, c_own, l_own, r_own, s_own, o_own),
    )
    for mine_first, deltas_ref, count_ref, left_ref, right_ref, start_ref, out_ref in jobs:
        if start_ref is None:
            acc_ref[...] = jnp.zeros_like(acc_ref)
        else:
            acc_ref[...] = start_ref[...]

        def step(k, carry, deltas_ref=deltas_ref, left_ref=left_ref, right_ref=right_ref, mine_first=mine_first):
            which = source_of(deltas_ref[k], parity, mine_first, phase)

            @pl.when(which < n_src)
            def _():
                left = left_ref[k]

                def run(src_ref):
                    for r in range(rows):
                        mixed_ref[pl.ds(r * width, width), :] = jnp.dot(
                            left, src_ref[r], preferred_element_type=jnp.float32
                        ).astype(jnp.bfloat16)

                for m, ref in enumerate(srcs):
                    pl.when(which == m)(functools.partial(run, ref))
                acc_ref[...] += lax.dot_general(
                    mixed_ref[...], right_ref[k], (((1,), (1,)), ((), ())), preferred_element_type=jnp.float32
                )

            return carry

        lax.fori_loop(0, jnp.minimum(count_ref[0], left_ref.shape[0]), step, 0)
        if phase == 2 and mine_first:
            offset = pl.multiple_of(parity * size, size)
            out_ref[pl.ds(offset, size), :] = acc_ref[...].astype(out_ref.dtype)
        else:
            out_ref[...] = acc_ref[...].astype(out_ref.dtype)


def apply_pairs(phase, sources, own_job, partner_job, starts=()):
    rows, width = sources[0].shape[0], sources[0].shape[1]
    size = rows * width
    left_ops, right_ops, deltas, counts = own_job
    left_p, right_p, deltas_p, counts_p = partner_job
    slots = left_ops.shape[0]
    vmem = pl.BlockSpec(memory_space=pltpu.VMEM)
    smem = pl.BlockSpec(memory_space=pltpu.SMEM)
    flops = 4 * slots * size * width * width // 2
    moved = 2 * (len(sources) * size * width + 4 * slots * width * width) + 16 * size * width
    if phase == 2:
        outs = (
            jax.ShapeDtypeStruct((2 * size, width), jnp.bfloat16),
            jax.ShapeDtypeStruct((size, width), jnp.bfloat16),
        )
    else:
        outs = (jax.ShapeDtypeStruct((size, width), jnp.float32),) * 2
    return pl.pallas_call(
        functools.partial(pairs_kernel, phase, len(sources)),
        out_shape=outs,
        in_specs=[smem] * 4 + [vmem] * (len(sources) + 4 + len(starts)),
        out_specs=(vmem, vmem),
        scratch_shapes=[
            pltpu.VMEM((size, width), jnp.float32),
            pltpu.VMEM((size, width), jnp.bfloat16),
        ],
        cost_estimate=pl.CostEstimate(flops=flops, bytes_accessed=moved, transcendentals=0),
    )(deltas, counts, deltas_p, counts_p, *sources, left_ops, right_ops, left_p, right_p, *starts)


def on_device(wave, left_ops, right_ops, deltas, counts):
    n = lax.axis_size("sector")
    me = lax.axis_index("sector")
    parity = me % 2
    own = wave[0]
    half = own.shape[0] // 2
    mine = lax.dynamic_slice_in_dim(own, parity * half, half, 0)
    other = lax.dynamic_slice_in_dim(own, (1 - parity) * half, half, 0)

    odd, even = range(1, n, 2), range(0, n, 2)
    near = [(j, j + 1) for j in odd if j + 1 < n] + [(j, j - 1) for j in even if j >= 2]
    far = [(j, j + 2) for j in odd if j + 2 < n] + [(j, j - 2) for j in even if j >= 2]
    partner = [(j, j ^ 1) for j in range(n)]

    from_far = lax.ppermute(mine, "sector", far)
    from_near = lax.ppermute(other, "sector", near)
    slots = left_ops.shape[0]
    packed = jnp.concatenate([other, left_ops, right_ops], 0)
    packed = lax.ppermute(packed, "sector", partner)
    from_partner = packed[:half]
    left_p = packed[half:half + slots]
    right_p = packed[half + slots:]
    ints = lax.ppermute(jnp.concatenate([deltas, counts]), "sector", partner)
    deltas_p, counts_p = ints[:slots], ints[slots:]
    own_job = (left_ops, right_ops, deltas, counts)
    partner_job = (left_p, right_p, deltas_p, counts_p)

    own_sum, partner_sum = apply_pairs(0, (mine, from_partner), own_job, partner_job)
    own_sum, partner_sum, from_near = lax.optimization_barrier((own_sum, partner_sum, from_near))
    own_sum, partner_sum = apply_pairs(1, (from_near,), own_job, partner_job, (own_sum, partner_sum))
    own_sum, partner_sum, from_far = lax.optimization_barrier((own_sum, partner_sum, from_far))
    out, partner_half = apply_pairs(2, (from_far,), own_job, partner_job, (own_sum, partner_sum))

    returned = lax.ppermute(partner_half.reshape((half,) + own.shape[1:]), "sector", partner)
    out = lax.dynamic_update_slice_in_dim(out.reshape(own.shape), returned, (1 - parity) * half, 0)
    return out[None]


def solution(mesh):
    return jax.shard_map(
        on_device,
        mesh=mesh,
        in_specs=(
            P(("group", "sector"), None, None, None),
            P(("group", "sector"), None, None),
            P(("group", "sector"), None, None),
            P(("group", "sector")),
            P(("group", "sector")),
        ),
        out_specs=P(("group", "sector"), None, None, None),
        check_vma=False,
    )
```

```python
import functools

import jax
import jax.numpy as jnp
from jax import lax
from jax.experimental import pallas as pl
from jax.experimental.pallas import tpu as pltpu
from jax.sharding import PartitionSpec as P


def source_of(delta, parity, mine_first, phase):
    pos = jnp.clip(delta, -1, 1) + 1 + (parity if mine_first else 1 - parity)
    phys = jnp.where(parity == 0, pos + 1 - 2 * (pos % 2), (pos + 2) % 4)
    if phase == 0:
        return jnp.where(phys == 0, 0, jnp.where(phys == 3, 1, 2))
    return jnp.where(phys == phase, 0, 2)


def pairs_kernel(phase, jobs, n_src, *refs):
    njobs = len(jobs)
    ints = refs[:2 * njobs]
    srcs = refs[2 * njobs:2 * njobs + n_src]
    ops = refs[2 * njobs + n_src:4 * njobs + n_src]
    rest = refs[4 * njobs + n_src:]
    starts = rest[:njobs] if phase > 0 else (None,) * njobs
    rest = rest[njobs:] if phase > 0 else rest
    outs, (acc_ref, mixed_ref) = rest[:njobs], rest[njobs:]
    rows, width = srcs[0].shape[0], srcs[0].shape[1]
    size = rows * width
    parity = lax.axis_index("sector") % 2
    for j, mine_first in enumerate(jobs):
        deltas_ref, count_ref = ints[2 * j], ints[2 * j + 1]
        left_ref, right_ref = ops[2 * j], ops[2 * j + 1]
        start_ref, out_ref = starts[j], outs[j]
        if start_ref is None:
            acc_ref[...] = jnp.zeros_like(acc_ref)
        else:
            acc_ref[...] = start_ref[...]

        def step(k, carry, deltas_ref=deltas_ref, left_ref=left_ref, right_ref=right_ref, mine_first=mine_first):
            which = source_of(deltas_ref[k], parity, mine_first, phase)

            @pl.when(which < n_src)
            def _():
                left = left_ref[k]

                def run(src_ref):
                    for r in range(rows):
                        mixed_ref[pl.ds(r * width, width), :] = jnp.dot(
                            left, src_ref[r], preferred_element_type=jnp.float32
                        ).astype(jnp.bfloat16)

                for m, ref in enumerate(srcs):
                    pl.when(which == m)(functools.partial(run, ref))
                acc_ref[...] += lax.dot_general(
                    mixed_ref[...], right_ref[k], (((1,), (1,)), ((), ())), preferred_element_type=jnp.float32
                )

            return carry

        lax.fori_loop(0, jnp.minimum(count_ref[0], left_ref.shape[0]), step, 0)
        if phase > 0 and mine_first:
            offset = pl.multiple_of(parity * size, size)
            out_ref[pl.ds(offset, size), :] = acc_ref[...].astype(out_ref.dtype)
        else:
            out_ref[...] = acc_ref[...].astype(out_ref.dtype)


def apply_pairs(phase, sources, jobs, starts=()):
    rows, width = sources[0].shape[0], sources[0].shape[1]
    size = rows * width
    slots = jobs[0][1][0].shape[0]
    vmem = pl.BlockSpec(memory_space=pltpu.VMEM)
    smem = pl.BlockSpec(memory_space=pltpu.SMEM)
    flops = 2 * slots * size * width * width * len(jobs) // 3
    moved = 2 * (len(sources) * size * width + 2 * len(jobs) * slots * width * width) + 8 * len(jobs) * size * width
    outs = []
    for is_own, _ in jobs:
        if phase == 0:
            outs.append(jax.ShapeDtypeStruct((size, width), jnp.float32))
        else:
            outs.append(jax.ShapeDtypeStruct(((2 if is_own else 1) * size, width), jnp.bfloat16))
    ints = [x for _, (l, r, d, c) in jobs for x in (d, c)]
    ops = [x for _, (l, r, d, c) in jobs for x in (l, r)]
    return pl.pallas_call(
        functools.partial(pairs_kernel, phase, tuple(o for o, _ in jobs), len(sources)),
        out_shape=tuple(outs),
        in_specs=[smem] * len(ints) + [vmem] * (len(sources) + len(ops) + len(starts)),
        out_specs=tuple(vmem for _ in outs),
        scratch_shapes=[
            pltpu.VMEM((size, width), jnp.float32),
            pltpu.VMEM((size, width), jnp.bfloat16),
        ],
        cost_estimate=pl.CostEstimate(flops=flops, bytes_accessed=moved, transcendentals=0),
    )(*ints, *sources, *ops, *starts)


def on_device(wave, left_ops, right_ops, deltas, counts):
    n = lax.axis_size("sector")
    me = lax.axis_index("sector")
    parity = me % 2
    own = wave[0]
    half = own.shape[0] // 2
    mine = lax.dynamic_slice_in_dim(own, parity * half, half, 0)
    other = lax.dynamic_slice_in_dim(own, (1 - parity) * half, half, 0)

    odd, even = range(1, n, 2), range(0, n, 2)
    near = [(j, j + 1) for j in odd if j + 1 < n] + [(j, j - 1) for j in even if j >= 2]
    far = [(j, j + 2) for j in odd if j + 2 < n] + [(j, j - 2) for j in even if j >= 2]
    partner = [(j, j ^ 1) for j in range(n)]

    from_near = lax.ppermute(other, "sector", near)
    from_far = lax.ppermute(mine, "sector", far)
    from_partner = lax.ppermute(other, "sector", partner)

    left_p = lax.ppermute(left_ops, "sector", partner)
    right_p = lax.ppermute(right_ops, "sector", partner)
    deltas_p = lax.ppermute(deltas, "sector", partner)
    counts_p = lax.ppermute(counts, "sector", partner)
    own_job = (left_ops, right_ops, deltas, counts)
    partner_job = (left_p, right_p, deltas_p, counts_p)

    partner_sum, own_sum = apply_pairs(0, (mine, from_partner), ((False, partner_job), (True, own_job)))
    own_sum, partner_sum, from_near = lax.optimization_barrier((own_sum, partner_sum, from_near))
    (out,) = apply_pairs(1, (from_near,), ((True, own_job),), (own_sum,))
    out, partner_sum, from_far = lax.optimization_barrier((out, partner_sum, from_far))
    (partner_half,) = apply_pairs(2, (from_far,), ((False, partner_job),), (partner_sum,))

    returned = lax.ppermute(partner_half.reshape((half,) + own.shape[1:]), "sector", partner)
    out = lax.dynamic_update_slice_in_dim(out.reshape(own.shape), returned, (1 - parity) * half, 0)
    return out[None]


def solution(mesh):
    return jax.shard_map(
        on_device,
        mesh=mesh,
        in_specs=(
            P(("group", "sector"), None, None, None),
            P(("group", "sector"), None, None),
            P(("group", "sector"), None, None),
            P(("group", "sector")),
            P(("group", "sector")),
        ),
        out_specs=P(("group", "sector"), None, None, None),
        check_vma=False,
    )
```

```python
import functools

import jax
import jax.numpy as jnp
from jax import lax
from jax.experimental import pallas as pl
from jax.experimental.pallas import tpu as pltpu
from jax.sharding import PartitionSpec as P


def source_of(delta, parity, own_job, phase):
    d = jnp.clip(delta, -1, 1)
    outer = 2 * parity - 1
    if own_job:
        if phase == 0:
            return jnp.where(d == 0, 0, jnp.where(d == -outer, 1, 2))
        return jnp.where(d == outer, 0, 2)
    if phase == 0:
        return jnp.where(d == 0, 1, jnp.where(d == outer, 0, 2))
    return jnp.where(d == -outer, 0, 2)


def pairs_kernel(phase, jobs, n_src, half, *refs):
    njobs = len(jobs)
    ints = refs[:2 * njobs]
    srcs = refs[2 * njobs:2 * njobs + n_src]
    ops = refs[2 * njobs + n_src:4 * njobs + n_src]
    rest = refs[4 * njobs + n_src:]
    starts = rest[:njobs] if phase > 0 else (None,) * njobs
    rest = rest[njobs:] if phase > 0 else rest
    outs, (acc_ref, mixed_ref) = rest[:njobs], rest[njobs:]
    width = srcs[0].shape[1]
    parity = lax.axis_index("sector") % 2
    for j, own_job in enumerate(jobs):
        deltas_ref, count_ref = ints[2 * j], ints[2 * j + 1]
        left_ref, right_ref = ops[2 * j], ops[2 * j + 1]
        start_ref, out_ref = starts[j], outs[j]
        first = 0 if (phase > 0 or own_job) else half
        if start_ref is None:
            acc_ref[...] = jnp.zeros_like(acc_ref)
        else:
            acc_ref[...] = start_ref[...]

        def step(k, carry, deltas_ref=deltas_ref, left_ref=left_ref, right_ref=right_ref, own_job=own_job, first=first):
            which = source_of(deltas_ref[k], parity, own_job, phase)

            @pl.when(which < n_src)
            def _():
                left = left_ref[k]

                def run(src_ref):
                    for r in range(half):
                        mixed_ref[pl.ds(r * width, width), :] = jnp.dot(
                            left, src_ref[first + r], preferred_element_type=jnp.float32
                        ).astype(jnp.bfloat16)

                for m, ref in enumerate(srcs):
                    pl.when(which == m)(functools.partial(run, ref))
                acc_ref[...] += lax.dot_general(
                    mixed_ref[...], right_ref[k], (((1,), (1,)), ((), ())), preferred_element_type=jnp.float32
                )

            return carry

        lax.fori_loop(0, jnp.minimum(count_ref[0], left_ref.shape[0]), step, 0)
        if phase > 0 and own_job:
            out_ref[pl.ds(0, half * width), :] = acc_ref[...].astype(out_ref.dtype)
        else:
            out_ref[...] = acc_ref[...].astype(out_ref.dtype)


def apply_pairs(phase, sources, jobs, half, starts=()):
    width = sources[0].shape[1]
    size = half * width
    slots = jobs[0][1][0].shape[0]
    vmem = pl.BlockSpec(memory_space=pltpu.VMEM)
    smem = pl.BlockSpec(memory_space=pltpu.SMEM)
    flops = 2 * slots * size * width * width * len(jobs) // 3
    moved = 2 * (len(sources) * size * width + 2 * len(jobs) * slots * width * width) + 8 * len(jobs) * size * width
    outs = []
    for is_own, _ in jobs:
        if phase == 0:
            outs.append(jax.ShapeDtypeStruct((size, width), jnp.float32))
        else:
            outs.append(jax.ShapeDtypeStruct(((2 if is_own else 1) * size, width), jnp.bfloat16))
    ints = [x for _, (l, r, d, c) in jobs for x in (d, c)]
    ops = [x for _, (l, r, d, c) in jobs for x in (l, r)]
    return pl.pallas_call(
        functools.partial(pairs_kernel, phase, tuple(o for o, _ in jobs), len(sources), half),
        out_shape=tuple(outs),
        in_specs=[smem] * len(ints) + [vmem] * (len(sources) + len(ops) + len(starts)),
        out_specs=tuple(vmem for _ in outs),
        scratch_shapes=[
            pltpu.VMEM((size, width), jnp.float32),
            pltpu.VMEM((size, width), jnp.bfloat16),
        ],
        cost_estimate=pl.CostEstimate(flops=flops, bytes_accessed=moved, transcendentals=0),
    )(*ints, *sources, *ops, *starts)


def on_device(wave, left_ops, right_ops, deltas, counts):
    n = lax.axis_size("sector")
    own = wave[0]
    half = own.shape[0] // 2

    odd, even = range(1, n, 2), range(0, n, 2)
    near = [(j, j + 1) for j in odd if j + 1 < n] + [(j, j - 1) for j in even if j >= 2]
    far = [(j, j + 2) for j in odd if j + 2 < n] + [(j, j - 2) for j in even if j >= 2]
    partner = [(j, j ^ 1) for j in range(n)]

    from_near = lax.ppermute(own[:half], "sector", near)
    from_far = lax.ppermute(own[half:], "sector", far)
    from_partner = lax.ppermute(own, "sector", partner)

    left_p = lax.ppermute(left_ops, "sector", partner)
    right_p = lax.ppermute(right_ops, "sector", partner)
    deltas_p = lax.ppermute(deltas, "sector", partner)
    counts_p = lax.ppermute(counts, "sector", partner)
    own_job = (left_ops, right_ops, deltas, counts)
    partner_job = (left_p, right_p, deltas_p, counts_p)

    partner_sum, own_sum = apply_pairs(0, (own, from_partner), ((False, partner_job), (True, own_job)), half)
    own_sum, partner_sum, from_near = lax.optimization_barrier((own_sum, partner_sum, from_near))
    (out,) = apply_pairs(1, (from_near,), ((True, own_job),), half, (own_sum,))
    out, partner_sum, from_far = lax.optimization_barrier((out, partner_sum, from_far))
    (partner_half,) = apply_pairs(2, (from_far,), ((False, partner_job),), half, (partner_sum,))

    returned = lax.ppermute(partner_half.reshape((half,) + own.shape[1:]), "sector", partner)
    out = lax.dynamic_update_slice_in_dim(out.reshape(own.shape), returned, half, 0)
    return out[None]


def solution(mesh):
    return jax.shard_map(
        on_device,
        mesh=mesh,
        in_specs=(
            P(("group", "sector"), None, None, None),
            P(("group", "sector"), None, None),
            P(("group", "sector"), None, None),
            P(("group", "sector")),
            P(("group", "sector")),
        ),
        out_specs=P(("group", "sector"), None, None, None),
        check_vma=False,
    )
```

```python
import functools

import jax
import jax.numpy as jnp
from jax import lax
from jax.experimental import pallas as pl
from jax.experimental.pallas import tpu as pltpu
from jax.sharding import PartitionSpec as P


def source_of(delta, parity, own_job, phase):
    d = jnp.clip(delta, -1, 1)
    outer = 2 * parity - 1
    if own_job:
        if phase == 0:
            return jnp.where(d == 0, 0, jnp.where(d == -outer, 1, 2))
        return jnp.where(d == outer, 0, 2)
    if phase == 0:
        return jnp.where(d == 0, 1, jnp.where(d == outer, 0, 2))
    return jnp.where(d == -outer, 0, 2)


def pairs_kernel(phase, jobs, n_src, half, *refs):
    njobs = len(jobs)
    ints = refs[:2 * njobs]
    srcs = refs[2 * njobs:2 * njobs + n_src]
    ops = refs[2 * njobs + n_src:4 * njobs + n_src]
    rest = refs[4 * njobs + n_src:]
    starts = rest[:njobs] if phase > 0 else (None,) * njobs
    rest = rest[njobs:] if phase > 0 else rest
    outs, (acc_ref, mixed_ref) = rest[:njobs], rest[njobs:]
    width = srcs[0].shape[1]
    parity = lax.axis_index("sector") % 2
    for j, own_job in enumerate(jobs):
        deltas_ref, count_ref = ints[2 * j], ints[2 * j + 1]
        left_ref, right_ref = ops[2 * j], ops[2 * j + 1]
        start_ref, out_ref = starts[j], outs[j]
        first = 0 if (phase > 0 or own_job) else half
        if start_ref is None:
            acc_ref[...] = jnp.zeros_like(acc_ref)
        else:
            acc_ref[...] = start_ref[...]

        def step(k, carry, deltas_ref=deltas_ref, left_ref=left_ref, right_ref=right_ref, own_job=own_job, first=first):
            which = source_of(deltas_ref[k], parity, own_job, phase)

            @pl.when(which < n_src)
            def _():
                left = left_ref[k]

                def run(src_ref):
                    for r in range(half):
                        mixed_ref[pl.ds(r * width, width), :] = jnp.dot(
                            left, src_ref[first + r], preferred_element_type=jnp.float32
                        ).astype(jnp.bfloat16)

                for m, ref in enumerate(srcs):
                    pl.when(which == m)(functools.partial(run, ref))
                acc_ref[...] += lax.dot_general(
                    mixed_ref[...], right_ref[k], (((1,), (1,)), ((), ())), preferred_element_type=jnp.float32
                )

            return carry

        lax.fori_loop(0, jnp.minimum(count_ref[0], left_ref.shape[0]), step, 0)
        if phase > 0 and own_job:
            out_ref[pl.ds(0, half * width), :] = acc_ref[...].astype(out_ref.dtype)
        else:
            out_ref[...] = acc_ref[...].astype(out_ref.dtype)


def apply_pairs(phase, sources, jobs, half, starts=()):
    width = sources[0].shape[1]
    size = half * width
    slots = jobs[0][1][0].shape[0]
    vmem = pl.BlockSpec(memory_space=pltpu.VMEM)
    smem = pl.BlockSpec(memory_space=pltpu.SMEM)
    flops = 2 * slots * size * width * width * len(jobs) // 3
    moved = 2 * (len(sources) * size * width + 2 * len(jobs) * slots * width * width) + 8 * len(jobs) * size * width
    outs = []
    for is_own, _ in jobs:
        if phase == 0:
            outs.append(jax.ShapeDtypeStruct((size, width), jnp.float32))
        else:
            outs.append(jax.ShapeDtypeStruct(((2 if is_own else 1) * size, width), jnp.bfloat16))
    ints = [x for _, (l, r, d, c) in jobs for x in (d, c)]
    ops = [x for _, (l, r, d, c) in jobs for x in (l, r)]
    return pl.pallas_call(
        functools.partial(pairs_kernel, phase, tuple(o for o, _ in jobs), len(sources), half),
        out_shape=tuple(outs),
        in_specs=[smem] * len(ints) + [vmem] * (len(sources) + len(ops) + len(starts)),
        out_specs=tuple(vmem for _ in outs),
        scratch_shapes=[
            pltpu.VMEM((size, width), jnp.float32),
            pltpu.VMEM((size, width), jnp.bfloat16),
        ],
        cost_estimate=pl.CostEstimate(flops=flops, bytes_accessed=moved, transcendentals=0),
    )(*ints, *sources, *ops, *starts)


def on_device(wave, left_ops, right_ops, deltas, counts):
    n = lax.axis_size("sector")
    own = wave[0]
    half = own.shape[0] // 2

    odd, even = range(1, n, 2), range(0, n, 2)
    near = [(j, j + 1) for j in odd if j + 1 < n] + [(j, j - 1) for j in even if j >= 2]
    far = [(j, j + 2) for j in odd if j + 2 < n] + [(j, j - 2) for j in even if j >= 2]
    partner = [(j, j ^ 1) for j in range(n)]

    from_near = lax.ppermute(own[:half], "sector", near)
    from_far = lax.ppermute(own[half:], "sector", far)
    from_partner = lax.ppermute(own, "sector", partner)

    slots = left_ops.shape[0]
    ops_p = lax.ppermute(jnp.concatenate([left_ops, right_ops], 0), "sector", partner)
    left_p, right_p = ops_p[:slots], ops_p[slots:]
    ints_p = lax.ppermute(jnp.concatenate([deltas, counts]), "sector", partner)
    deltas_p, counts_p = ints_p[:slots], ints_p[slots:]
    own_job = (left_ops, right_ops, deltas, counts)
    partner_job = (left_p, right_p, deltas_p, counts_p)

    partner_sum, own_sum = apply_pairs(0, (own, from_partner), ((False, partner_job), (True, own_job)), half)
    own_sum, partner_sum, from_near = lax.optimization_barrier((own_sum, partner_sum, from_near))
    (out,) = apply_pairs(1, (from_near,), ((True, own_job),), half, (own_sum,))
    out, partner_sum, from_far = lax.optimization_barrier((out, partner_sum, from_far))
    (partner_half,) = apply_pairs(2, (from_far,), ((False, partner_job),), half, (partner_sum,))

    returned = lax.ppermute(partner_half.reshape((half,) + own.shape[1:]), "sector", partner)
    out = lax.dynamic_update_slice_in_dim(out.reshape(own.shape), returned, half, 0)
    return out[None]


def solution(mesh):
    return jax.shard_map(
        on_device,
        mesh=mesh,
        in_specs=(
            P(("group", "sector"), None, None, None),
            P(("group", "sector"), None, None),
            P(("group", "sector"), None, None),
            P(("group", "sector")),
            P(("group", "sector")),
        ),
        out_specs=P(("group", "sector"), None, None, None),
        check_vma=False,
    )
```

```python
import functools

import jax
import jax.numpy as jnp
from jax import lax
from jax.experimental import pallas as pl
from jax.experimental.pallas import tpu as pltpu
from jax.sharding import PartitionSpec as P


def source_of(delta, parity, own_job, phase):
    d = jnp.clip(delta, -1, 1)
    outer = 2 * parity - 1
    if own_job:
        if phase == 0:
            return jnp.where(d == 0, 0, jnp.where(d == -outer, 1, 2))
        return jnp.where(d == outer, 0, 2)
    if phase == 0:
        return jnp.where(d == 0, 1, jnp.where(d == outer, 0, 2))
    return jnp.where(d == -outer, 0, 2)


def pairs_kernel(phase, jobs, n_src, half, *refs):
    njobs = len(jobs)
    ints = refs[:2 * njobs]
    srcs = refs[2 * njobs:2 * njobs + n_src]
    ops = refs[2 * njobs + n_src:4 * njobs + n_src]
    rest = refs[4 * njobs + n_src:]
    starts = rest[:njobs] if phase > 0 else (None,) * njobs
    rest = rest[njobs:] if phase > 0 else rest
    outs, (acc_ref, mixed_ref) = rest[:njobs], rest[njobs:]
    width = srcs[0].shape[1]
    parity = lax.axis_index("sector") % 2
    for j, own_job in enumerate(jobs):
        deltas_ref, count_ref = ints[2 * j], ints[2 * j + 1]
        left_ref, right_ref = ops[2 * j], ops[2 * j + 1]
        start_ref, out_ref = starts[j], outs[j]
        first = 0 if (phase > 0 or own_job) else half
        if start_ref is None:
            acc_ref[...] = jnp.zeros_like(acc_ref)
        else:
            acc_ref[...] = start_ref[...]

        def step(k, carry, deltas_ref=deltas_ref, left_ref=left_ref, right_ref=right_ref, own_job=own_job, first=first):
            which = source_of(deltas_ref[k], parity, own_job, phase)

            @pl.when(which < n_src)
            def _():
                left = left_ref[k]

                def run(src_ref):
                    for r in range(half):
                        mixed_ref[pl.ds(r * width, width), :] = jnp.dot(
                            left, src_ref[first + r], preferred_element_type=jnp.float32
                        ).astype(jnp.bfloat16)

                for m, ref in enumerate(srcs):
                    pl.when(which == m)(functools.partial(run, ref))
                acc_ref[...] += lax.dot_general(
                    mixed_ref[...], right_ref[k], (((1,), (1,)), ((), ())), preferred_element_type=jnp.float32
                )

            return carry

        lax.fori_loop(0, jnp.minimum(count_ref[0], left_ref.shape[0]), step, 0)
        if phase > 0 and own_job:
            out_ref[pl.ds(0, half * width), :] = acc_ref[...].astype(out_ref.dtype)
        else:
            out_ref[...] = acc_ref[...].astype(out_ref.dtype)


def apply_pairs(phase, sources, jobs, half, starts=()):
    width = sources[0].shape[1]
    size = half * width
    slots = jobs[0][1][0].shape[0]
    vmem = pl.BlockSpec(memory_space=pltpu.VMEM)
    smem = pl.BlockSpec(memory_space=pltpu.SMEM)
    flops = 2 * slots * size * width * width * len(jobs) // 3
    moved = 2 * (len(sources) * size * width + 2 * len(jobs) * slots * width * width) + 8 * len(jobs) * size * width
    outs = []
    for is_own, _ in jobs:
        if phase == 0:
            outs.append(jax.ShapeDtypeStruct((size, width), jnp.float32))
        else:
            outs.append(jax.ShapeDtypeStruct(((2 if is_own else 1) * size, width), jnp.bfloat16))
    ints = [x for _, (l, r, d, c) in jobs for x in (d, c)]
    ops = [x for _, (l, r, d, c) in jobs for x in (l, r)]
    return pl.pallas_call(
        functools.partial(pairs_kernel, phase, tuple(o for o, _ in jobs), len(sources), half),
        out_shape=tuple(outs),
        in_specs=[smem] * len(ints) + [vmem] * (len(sources) + len(ops) + len(starts)),
        out_specs=tuple(vmem for _ in outs),
        scratch_shapes=[
            pltpu.VMEM((size, width), jnp.float32),
            pltpu.VMEM((size, width), jnp.bfloat16),
        ],
        cost_estimate=pl.CostEstimate(flops=flops, bytes_accessed=moved, transcendentals=0),
    )(*ints, *sources, *ops, *starts)


def on_device(wave, left_ops, right_ops, deltas, counts):
    n = lax.axis_size("sector")
    own = wave[0]
    half = own.shape[0] // 2

    odd, even = range(1, n, 2), range(0, n, 2)
    near = [(j, j + 1) for j in odd if j + 1 < n] + [(j, j - 1) for j in even if j >= 2]
    far = [(j, j + 2) for j in odd if j + 2 < n] + [(j, j - 2) for j in even if j >= 2]
    partner = [(j, j ^ 1) for j in range(n)]

    from_near = lax.ppermute(own[:half], "sector", near)
    from_far = lax.ppermute(own[half:], "sector", far)
    from_partner = lax.ppermute(own, "sector", partner)

    slots = left_ops.shape[0]
    ops_p = lax.ppermute(jnp.concatenate([left_ops, right_ops], 0), "sector", partner)
    left_p, right_p = ops_p[:slots], ops_p[slots:]
    ints_p = lax.ppermute(jnp.concatenate([deltas, counts]), "sector", partner)
    deltas_p, counts_p = ints_p[:slots], ints_p[slots:]
    own_job = (left_ops, right_ops, deltas, counts)
    partner_job = (left_p, right_p, deltas_p, counts_p)

    partner_sum, own_sum = apply_pairs(0, (own, from_partner), ((False, partner_job), (True, own_job)), half)
    own_sum, partner_sum, from_far = lax.optimization_barrier((own_sum, partner_sum, from_far))
    (partner_half,) = apply_pairs(2, (from_far,), ((False, partner_job),), half, (partner_sum,))
    own_sum, partner_half, from_near = lax.optimization_barrier((own_sum, partner_half, from_near))
    returned = lax.ppermute(partner_half.reshape((half,) + own.shape[1:]), "sector", partner)
    (out,) = apply_pairs(1, (from_near,), ((True, own_job),), half, (own_sum,))
    out = lax.dynamic_update_slice_in_dim(out.reshape(own.shape), returned, half, 0)
    return out[None]


def solution(mesh):
    return jax.shard_map(
        on_device,
        mesh=mesh,
        in_specs=(
            P(("group", "sector"), None, None, None),
            P(("group", "sector"), None, None),
            P(("group", "sector"), None, None),
            P(("group", "sector")),
            P(("group", "sector")),
        ),
        out_specs=P(("group", "sector"), None, None, None),
        check_vma=False,
    )
```

```python
import functools

import jax
import jax.numpy as jnp
from jax import lax
from jax.experimental import pallas as pl
from jax.experimental.pallas import tpu as pltpu
from jax.sharding import PartitionSpec as P


def source_of(delta, parity, own_job, phase):
    d = jnp.clip(delta, -1, 1)
    outer = 2 * parity - 1
    if own_job:
        if phase == 0:
            return jnp.where(d == 0, 0, jnp.where(d == -outer, 1, 2))
        return jnp.where(d == outer, 0, 2)
    if phase == 0:
        return jnp.where(d == 0, 1, jnp.where(d == outer, 0, 2))
    return jnp.where(d == -outer, 0, 2)


def pairs_kernel(phase, jobs, n_src, half, *refs):
    njobs = len(jobs)
    ints = refs[:2 * njobs]
    srcs = refs[2 * njobs:2 * njobs + n_src]
    ops = refs[2 * njobs + n_src:4 * njobs + n_src]
    rest = refs[4 * njobs + n_src:]
    starts = rest[:njobs] if phase > 0 else (None,) * njobs
    rest = rest[njobs:] if phase > 0 else rest
    outs, (acc_ref, mixed_ref) = rest[:njobs], rest[njobs:]
    width = srcs[0].shape[1]
    parity = lax.axis_index("sector") % 2
    for j, own_job in enumerate(jobs):
        deltas_ref, count_ref = ints[2 * j], ints[2 * j + 1]
        left_ref, right_ref = ops[2 * j], ops[2 * j + 1]
        start_ref, out_ref = starts[j], outs[j]
        first = 0 if (phase > 0 or own_job) else half
        if start_ref is None:
            acc_ref[...] = jnp.zeros_like(acc_ref)
        else:
            acc_ref[...] = start_ref[...]

        def step(k, carry, deltas_ref=deltas_ref, left_ref=left_ref, right_ref=right_ref, own_job=own_job, first=first):
            which = source_of(deltas_ref[k], parity, own_job, phase)

            @pl.when(which < n_src)
            def _():
                left = left_ref[k]

                def run(src_ref):
                    for r in range(half):
                        mixed_ref[pl.ds(r * width, width), :] = jnp.dot(
                            left, src_ref[first + r], preferred_element_type=jnp.float32
                        ).astype(jnp.bfloat16)

                for m, ref in enumerate(srcs):
                    pl.when(which == m)(functools.partial(run, ref))
                acc_ref[...] += lax.dot_general(
                    mixed_ref[...], right_ref[k], (((1,), (1,)), ((), ())), preferred_element_type=jnp.float32
                )

            return carry

        lax.fori_loop(0, jnp.minimum(count_ref[0], left_ref.shape[0]), step, 0)
        if phase > 0 and own_job:
            out_ref[pl.ds(0, half * width), :] = acc_ref[...].astype(out_ref.dtype)
        else:
            out_ref[...] = acc_ref[...].astype(out_ref.dtype)


def apply_pairs(phase, sources, jobs, half, starts=()):
    width = sources[0].shape[1]
    size = half * width
    slots = jobs[0][1][0].shape[0]
    vmem = pl.BlockSpec(memory_space=pltpu.VMEM)
    smem = pl.BlockSpec(memory_space=pltpu.SMEM)
    flops = 2 * slots * size * width * width * len(jobs) // 3
    moved = 2 * (len(sources) * size * width + 2 * len(jobs) * slots * width * width) + 8 * len(jobs) * size * width
    outs = []
    for is_own, _ in jobs:
        if phase == 0:
            outs.append(jax.ShapeDtypeStruct((size, width), jnp.float32))
        else:
            outs.append(jax.ShapeDtypeStruct(((2 if is_own else 1) * size, width), jnp.bfloat16))
    ints = [x for _, (l, r, d, c) in jobs for x in (d, c)]
    ops = [x for _, (l, r, d, c) in jobs for x in (l, r)]
    return pl.pallas_call(
        functools.partial(pairs_kernel, phase, tuple(o for o, _ in jobs), len(sources), half),
        out_shape=tuple(outs),
        in_specs=[smem] * len(ints) + [vmem] * (len(sources) + len(ops) + len(starts)),
        out_specs=tuple(vmem for _ in outs),
        scratch_shapes=[
            pltpu.VMEM((size, width), jnp.float32),
            pltpu.VMEM((size, width), jnp.bfloat16),
        ],
        cost_estimate=pl.CostEstimate(flops=flops, bytes_accessed=moved, transcendentals=0),
    )(*ints, *sources, *ops, *starts)


def on_device(wave, left_ops, right_ops, deltas, counts):
    n = lax.axis_size("sector")
    own = wave[0]
    half = own.shape[0] // 2

    odd, even = range(1, n, 2), range(0, n, 2)
    near = [(j, j + 1) for j in odd if j + 1 < n] + [(j, j - 1) for j in even if j >= 2]
    far = [(j, j + 2) for j in odd if j + 2 < n] + [(j, j - 2) for j in even if j >= 2]
    partner = [(j, j ^ 1) for j in range(n)]

    from_near = lax.ppermute(own[:half], "sector", near)
    from_far = lax.ppermute(own[half:], "sector", far)
    from_partner = lax.ppermute(own, "sector", partner)

    slots = left_ops.shape[0]
    ops_p = lax.ppermute(jnp.concatenate([left_ops, right_ops], 0), "sector", partner)
    left_p, right_p = ops_p[:slots], ops_p[slots:]
    ints_p = lax.ppermute(jnp.concatenate([deltas, counts]), "sector", partner)
    deltas_p, counts_p = ints_p[:slots], ints_p[slots:]
    own_job = (left_ops, right_ops, deltas, counts)
    partner_job = (left_p, right_p, deltas_p, counts_p)

    partner_sum, own_sum = apply_pairs(0, (own, from_partner), ((False, partner_job), (True, own_job)), half)
    own_sum, partner_sum, from_far = lax.optimization_barrier((own_sum, partner_sum, from_far))
    (partner_half,) = apply_pairs(2, (from_far,), ((False, partner_job),), half, (partner_sum,))
    returned = lax.ppermute(partner_half.reshape((half,) + own.shape[1:]), "sector", partner)
    own_sum, partner_half, from_near = lax.optimization_barrier((own_sum, partner_half, from_near))
    (out,) = apply_pairs(1, (from_near,), ((True, own_job),), half, (own_sum,))
    out = lax.dynamic_update_slice_in_dim(out.reshape(own.shape), returned, half, 0)
    return out[None]


def solution(mesh):
    return jax.shard_map(
        on_device,
        mesh=mesh,
        in_specs=(
            P(("group", "sector"), None, None, None),
            P(("group", "sector"), None, None),
            P(("group", "sector"), None, None),
            P(("group", "sector")),
            P(("group", "sector")),
        ),
        out_specs=P(("group", "sector"), None, None, None),
        check_vma=False,
    )
```

```python
import functools

import jax
import jax.numpy as jnp
from jax import lax
from jax.experimental import pallas as pl
from jax.experimental.pallas import tpu as pltpu
from jax.sharding import PartitionSpec as P


def source_of(delta, parity, own_job, phase):
    d = jnp.clip(delta, -1, 1)
    outer = 2 * parity - 1
    if own_job:
        if phase == 0:
            return jnp.where(d == 0, 0, jnp.where(d == -outer, 1, 2))
        return jnp.where(d == outer, 0, 2)
    if phase == 0:
        return jnp.where(d == 0, 1, jnp.where(d == outer, 0, 2))
    return jnp.where(d == -outer, 0, 2)


def pairs_kernel(phase, jobs, n_src, *refs):
    njobs = len(jobs)
    ints = refs[:2 * njobs]
    srcs = refs[2 * njobs:2 * njobs + n_src]
    ops = refs[2 * njobs + n_src:4 * njobs + n_src]
    rest = refs[4 * njobs + n_src:]
    starts = rest[:njobs] if phase > 0 else (None,) * njobs
    rest = rest[njobs:] if phase > 0 else rest
    outs, (acc_ref, mixed_ref) = rest[:njobs], rest[njobs:]
    width = srcs[0].shape[1]
    parity = lax.axis_index("sector") % 2
    for j, (own_job, nroots, first) in enumerate(jobs):
        deltas_ref, count_ref = ints[2 * j], ints[2 * j + 1]
        left_ref, right_ref = ops[2 * j], ops[2 * j + 1]
        start_ref, out_ref = starts[j], outs[j]
        size = nroots * width
        if start_ref is None:
            acc_ref[pl.ds(0, size), :] = jnp.zeros((size, width), jnp.float32)
        else:
            acc_ref[pl.ds(0, size), :] = start_ref[...]

        def step(k, carry, deltas_ref=deltas_ref, left_ref=left_ref, right_ref=right_ref, own_job=own_job, first=first,
                 nroots=nroots, size=size):
            which = source_of(deltas_ref[k], parity, own_job, phase)

            @pl.when(which < n_src)
            def _():
                left = left_ref[k]

                def run(src_ref):
                    for r in range(nroots):
                        mixed_ref[pl.ds(r * width, width), :] = jnp.dot(
                            left, src_ref[first + r], preferred_element_type=jnp.float32
                        ).astype(jnp.bfloat16)

                for m, ref in enumerate(srcs):
                    pl.when(which == m)(functools.partial(run, ref))
                acc_ref[pl.ds(0, size), :] += lax.dot_general(
                    mixed_ref[pl.ds(0, size), :], right_ref[k], (((1,), (1,)), ((), ())),
                    preferred_element_type=jnp.float32,
                )

            return carry

        lax.fori_loop(0, jnp.minimum(count_ref[0], left_ref.shape[0]), step, 0)
        if phase > 0 and own_job:
            out_ref[pl.ds(0, size), :] = acc_ref[pl.ds(0, size), :].astype(out_ref.dtype)
        else:
            out_ref[...] = acc_ref[pl.ds(0, size), :].astype(out_ref.dtype)


def apply_pairs(phase, sources, jobs, starts=()):
    width = sources[0].shape[1]
    slots = jobs[0][3][0].shape[0]
    biggest = max(j[1] for j in jobs) * width
    vmem = pl.BlockSpec(memory_space=pltpu.VMEM)
    smem = pl.BlockSpec(memory_space=pltpu.SMEM)
    rows = sum(j[1] for j in jobs) * width
    flops = 2 * slots * rows * width * width // 3
    moved = 2 * (len(sources) * biggest * width + 4 * len(jobs) * slots * width * width) + 8 * rows * width
    outs = []
    for is_own, nroots, _, _ in jobs:
        if phase == 0:
            outs.append(jax.ShapeDtypeStruct((nroots * width, width), jnp.float32))
        else:
            outs.append(jax.ShapeDtypeStruct((nroots * width, width), jnp.bfloat16))
    ints = [x for _, _, _, (l, r, d, c) in jobs for x in (d, c)]
    ops = [x for _, _, _, (l, r, d, c) in jobs for x in (l, r)]
    return pl.pallas_call(
        functools.partial(pairs_kernel, phase, tuple((o, n, f) for o, n, f, _ in jobs), len(sources)),
        out_shape=tuple(outs),
        in_specs=[smem] * len(ints) + [vmem] * (len(sources) + len(ops) + len(starts)),
        out_specs=tuple(vmem for _ in outs),
        scratch_shapes=[
            pltpu.VMEM((biggest, width), jnp.float32),
            pltpu.VMEM((biggest, width), jnp.bfloat16),
        ],
        cost_estimate=pl.CostEstimate(flops=flops, bytes_accessed=moved, transcendentals=0),
    )(*ints, *sources, *ops, *starts)


def on_device(wave, left_ops, right_ops, deltas, counts):
    n = lax.axis_size("sector")
    own = wave[0]
    roots = own.shape[0]
    first = roots * 3 // 8
    rest = roots - first

    odd, even = range(1, n, 2), range(0, n, 2)
    near = [(j, j + 1) for j in odd if j + 1 < n] + [(j, j - 1) for j in even if j >= 2]
    far = [(j, j + 2) for j in odd if j + 2 < n] + [(j, j - 2) for j in even if j >= 2]
    partner = [(j, j ^ 1) for j in range(n)]

    from_near = lax.ppermute(own[:first], "sector", near)
    from_far = lax.ppermute(own[first:], "sector", far)
    from_partner = lax.ppermute(own, "sector", partner)

    slots = left_ops.shape[0]
    ops_p = lax.ppermute(jnp.concatenate([left_ops, right_ops], 0), "sector", partner)
    left_p, right_p = ops_p[:slots], ops_p[slots:]
    ints_p = lax.ppermute(jnp.concatenate([deltas, counts]), "sector", partner)
    deltas_p, counts_p = ints_p[:slots], ints_p[slots:]
    own_job = (left_ops, right_ops, deltas, counts)
    partner_job = (left_p, right_p, deltas_p, counts_p)

    partner_sum, own_sum = apply_pairs(
        0, (own, from_partner), ((False, rest, first, partner_job), (True, first, 0, own_job))
    )
    own_sum, partner_sum, from_far = lax.optimization_barrier((own_sum, partner_sum, from_far))
    (partner_part,) = apply_pairs(2, (from_far,), ((False, rest, 0, partner_job),), (partner_sum,))
    own_sum, partner_part, from_near = lax.optimization_barrier((own_sum, partner_part, from_near))
    returned = lax.ppermute(partner_part.reshape((rest,) + own.shape[1:]), "sector", partner)
    (out,) = apply_pairs(1, (from_near,), ((True, first, 0, own_job),), (own_sum,))
    out = jnp.concatenate([out.reshape((first,) + own.shape[1:]), returned], 0)
    return out[None]


def solution(mesh):
    return jax.shard_map(
        on_device,
        mesh=mesh,
        in_specs=(
            P(("group", "sector"), None, None, None),
            P(("group", "sector"), None, None),
            P(("group", "sector"), None, None),
            P(("group", "sector")),
            P(("group", "sector")),
        ),
        out_specs=P(("group", "sector"), None, None, None),
        check_vma=False,
    )
```

```python
import functools

import jax
import jax.numpy as jnp
from jax import lax
from jax.experimental import pallas as pl
from jax.experimental.pallas import tpu as pltpu
from jax.sharding import PartitionSpec as P


def source_of(delta, parity, own_job, phase):
    d = jnp.clip(delta, -1, 1)
    outer = 2 * parity - 1
    if own_job:
        if phase == 0:
            return jnp.where(d == 0, 0, jnp.where(d == -outer, 1, 2))
        return jnp.where(d == outer, 0, 2)
    if phase == 0:
        return jnp.where(d == 0, 1, jnp.where(d == outer, 0, 2))
    return jnp.where(d == -outer, 0, 2)


def pairs_kernel(phase, jobs, n_src, half, *refs):
    njobs = len(jobs)
    ints = refs[:2 * njobs]
    srcs = refs[2 * njobs:2 * njobs + n_src]
    ops = refs[2 * njobs + n_src:4 * njobs + n_src]
    rest = refs[4 * njobs + n_src:]
    starts = rest[:njobs] if phase > 0 else (None,) * njobs
    rest = rest[njobs:] if phase > 0 else rest
    outs, (acc_ref, mixed_ref) = rest[:njobs], rest[njobs:]
    width = srcs[0].shape[1]
    parity = lax.axis_index("sector") % 2
    for j, own_job in enumerate(jobs):
        deltas_ref, count_ref = ints[2 * j], ints[2 * j + 1]
        left_ref, right_ref = ops[2 * j], ops[2 * j + 1]
        start_ref, out_ref = starts[j], outs[j]
        first = 0 if (phase > 0 or own_job) else half
        if start_ref is None:
            acc_ref[...] = jnp.zeros_like(acc_ref)
        else:
            acc_ref[...] = start_ref[...]

        def step(k, carry, deltas_ref=deltas_ref, left_ref=left_ref, right_ref=right_ref, own_job=own_job, first=first):
            which = source_of(deltas_ref[k], parity, own_job, phase)

            @pl.when(which < n_src)
            def _():
                left = left_ref[k]

                def run(src_ref):
                    for r in range(half):
                        mixed_ref[pl.ds(r * width, width), :] = jnp.dot(
                            left, src_ref[first + r], preferred_element_type=jnp.float32
                        ).astype(jnp.bfloat16)

                for m, ref in enumerate(srcs):
                    pl.when(which == m)(functools.partial(run, ref))
                acc_ref[...] += jnp.dot(mixed_ref[...], right_ref[k], preferred_element_type=jnp.float32)

            return carry

        lax.fori_loop(0, jnp.minimum(count_ref[0], left_ref.shape[0]), step, 0)
        if phase > 0 and own_job:
            out_ref[pl.ds(0, half * width), :] = acc_ref[...].astype(out_ref.dtype)
        else:
            out_ref[...] = acc_ref[...].astype(out_ref.dtype)


def apply_pairs(phase, sources, jobs, half, starts=()):
    width = sources[0].shape[1]
    size = half * width
    slots = jobs[0][1][0].shape[0]
    vmem = pl.BlockSpec(memory_space=pltpu.VMEM)
    smem = pl.BlockSpec(memory_space=pltpu.SMEM)
    flops = 2 * slots * size * width * width * len(jobs) // 3
    moved = 2 * (len(sources) * size * width + 2 * len(jobs) * slots * width * width) + 8 * len(jobs) * size * width
    outs = []
    for is_own, _ in jobs:
        if phase == 0:
            outs.append(jax.ShapeDtypeStruct((size, width), jnp.float32))
        else:
            outs.append(jax.ShapeDtypeStruct(((2 if is_own else 1) * size, width), jnp.bfloat16))
    ints = [x for _, (l, r, d, c) in jobs for x in (d, c)]
    ops = [x for _, (l, r, d, c) in jobs for x in (l, r)]
    return pl.pallas_call(
        functools.partial(pairs_kernel, phase, tuple(o for o, _ in jobs), len(sources), half),
        out_shape=tuple(outs),
        in_specs=[smem] * len(ints) + [vmem] * (len(sources) + len(ops) + len(starts)),
        out_specs=tuple(vmem for _ in outs),
        scratch_shapes=[
            pltpu.VMEM((size, width), jnp.float32),
            pltpu.VMEM((size, width), jnp.bfloat16),
        ],
        cost_estimate=pl.CostEstimate(flops=flops, bytes_accessed=moved, transcendentals=0),
    )(*ints, *sources, *ops, *starts)


def on_device(wave, left_ops, right_ops, deltas, counts):
    n = lax.axis_size("sector")
    own = wave[0]
    half = own.shape[0] // 2

    odd, even = range(1, n, 2), range(0, n, 2)
    near = [(j, j + 1) for j in odd if j + 1 < n] + [(j, j - 1) for j in even if j >= 2]
    far = [(j, j + 2) for j in odd if j + 2 < n] + [(j, j - 2) for j in even if j >= 2]
    partner = [(j, j ^ 1) for j in range(n)]

    from_near = lax.ppermute(own[:half], "sector", near)
    from_far = lax.ppermute(own[half:], "sector", far)
    from_partner = lax.ppermute(own, "sector", partner)

    slots = left_ops.shape[0]
    right_ops = jnp.swapaxes(right_ops, 1, 2)
    ops_p = lax.ppermute(jnp.concatenate([left_ops, right_ops], 0), "sector", partner)
    left_p, right_p = ops_p[:slots], ops_p[slots:]
    ints_p = lax.ppermute(jnp.concatenate([deltas, counts]), "sector", partner)
    deltas_p, counts_p = ints_p[:slots], ints_p[slots:]
    own_job = (left_ops, right_ops, deltas, counts)
    partner_job = (left_p, right_p, deltas_p, counts_p)

    partner_sum, own_sum = apply_pairs(0, (own, from_partner), ((False, partner_job), (True, own_job)), half)
    own_sum, partner_sum, from_far = lax.optimization_barrier((own_sum, partner_sum, from_far))
    (partner_half,) = apply_pairs(2, (from_far,), ((False, partner_job),), half, (partner_sum,))
    own_sum, partner_half, from_near = lax.optimization_barrier((own_sum, partner_half, from_near))
    returned = lax.ppermute(partner_half.reshape((half,) + own.shape[1:]), "sector", partner)
    (out,) = apply_pairs(1, (from_near,), ((True, own_job),), half, (own_sum,))
    out = lax.dynamic_update_slice_in_dim(out.reshape(own.shape), returned, half, 0)
    return out[None]


def solution(mesh):
    return jax.shard_map(
        on_device,
        mesh=mesh,
        in_specs=(
            P(("group", "sector"), None, None, None),
            P(("group", "sector"), None, None),
            P(("group", "sector"), None, None),
            P(("group", "sector")),
            P(("group", "sector")),
        ),
        out_specs=P(("group", "sector"), None, None, None),
        check_vma=False,
    )
```

```python
import functools

import jax
import jax.numpy as jnp
from jax import lax
from jax.experimental import pallas as pl
from jax.experimental.pallas import tpu as pltpu
from jax.sharding import PartitionSpec as P


def source_of(delta, parity, own_job, phase):
    d = jnp.clip(delta, -1, 1)
    outer = 2 * parity - 1
    if own_job:
        if phase == 0:
            return jnp.where(d == 0, 0, jnp.where(d == -outer, 1, 2))
        return jnp.where(d == outer, 0, 2)
    if phase == 0:
        return jnp.where(d == 0, 1, jnp.where(d == outer, 0, 2))
    return jnp.where(d == -outer, 0, 2)


def pairs_kernel(phase, jobs, n_src, half, *refs):
    njobs = len(jobs)
    ints = refs[:2 * njobs]
    srcs = refs[2 * njobs:2 * njobs + n_src]
    ops = refs[2 * njobs + n_src:4 * njobs + n_src]
    rest = refs[4 * njobs + n_src:]
    starts = rest[:njobs] if phase > 0 else (None,) * njobs
    rest = rest[njobs:] if phase > 0 else rest
    outs, (acc_ref, mixed_ref) = rest[:njobs], rest[njobs:]
    width = srcs[0].shape[1]
    parity = lax.axis_index("sector") % 2
    for j, own_job in enumerate(jobs):
        deltas_ref, count_ref = ints[2 * j], ints[2 * j + 1]
        left_ref, right_ref = ops[2 * j], ops[2 * j + 1]
        start_ref, out_ref = starts[j], outs[j]
        first = 0 if (phase > 0 or own_job) else half
        if start_ref is None:
            acc_ref[...] = jnp.zeros_like(acc_ref)
        else:
            acc_ref[...] = start_ref[...]

        def step(k, carry, deltas_ref=deltas_ref, left_ref=left_ref, right_ref=right_ref, own_job=own_job, first=first):
            which = source_of(deltas_ref[k], parity, own_job, phase)

            @pl.when(which < n_src)
            def _():
                left = left_ref[k]

                def run(src_ref):
                    for r in range(half):
                        mixed_ref[pl.ds(r * width, width), :] = jnp.dot(
                            left, src_ref[first + r], preferred_element_type=jnp.float32
                        ).astype(jnp.bfloat16)

                for m, ref in enumerate(srcs):
                    pl.when(which == m)(functools.partial(run, ref))
                acc_ref[...] += lax.dot_general(
                    mixed_ref[...], right_ref[k], (((1,), (1,)), ((), ())), preferred_element_type=jnp.float32
                )

            return carry

        lax.fori_loop(0, jnp.minimum(count_ref[0], left_ref.shape[0]), step, 0)
        out_ref[...] = acc_ref[...].astype(out_ref.dtype)


def apply_pairs(phase, sources, jobs, half, starts=()):
    width = sources[0].shape[1]
    size = half * width
    slots = jobs[0][1][0].shape[0]
    vmem = pl.BlockSpec(memory_space=pltpu.VMEM)
    smem = pl.BlockSpec(memory_space=pltpu.SMEM)
    flops = 2 * slots * size * width * width * len(jobs) // 3
    moved = 2 * (len(sources) * size * width + 2 * len(jobs) * slots * width * width) + 8 * len(jobs) * size * width
    outs = []
    for is_own, _ in jobs:
        if phase == 0:
            outs.append(jax.ShapeDtypeStruct((size, width), jnp.float32))
        else:
            outs.append(jax.ShapeDtypeStruct((size, width), jnp.bfloat16))
    ints = [x for _, (l, r, d, c) in jobs for x in (d, c)]
    ops = [x for _, (l, r, d, c) in jobs for x in (l, r)]
    return pl.pallas_call(
        functools.partial(pairs_kernel, phase, tuple(o for o, _ in jobs), len(sources), half),
        out_shape=tuple(outs),
        in_specs=[smem] * len(ints) + [vmem] * (len(sources) + len(ops) + len(starts)),
        out_specs=tuple(vmem for _ in outs),
        scratch_shapes=[
            pltpu.VMEM((size, width), jnp.float32),
            pltpu.VMEM((size, width), jnp.bfloat16),
        ],
        cost_estimate=pl.CostEstimate(flops=flops, bytes_accessed=moved, transcendentals=0),
    )(*ints, *sources, *ops, *starts)


def on_device(wave, left_ops, right_ops, deltas, counts):
    n = lax.axis_size("sector")
    own = wave[0]
    half = own.shape[0] // 2

    odd, even = range(1, n, 2), range(0, n, 2)
    near = [(j, j + 1) for j in odd if j + 1 < n] + [(j, j - 1) for j in even if j >= 2]
    far = [(j, j + 2) for j in odd if j + 2 < n] + [(j, j - 2) for j in even if j >= 2]
    partner = [(j, j ^ 1) for j in range(n)]

    from_near = lax.ppermute(own[:half], "sector", near)
    from_far = lax.ppermute(own[half:], "sector", far)
    from_partner = lax.ppermute(own, "sector", partner)

    slots = left_ops.shape[0]
    ops_p = lax.ppermute(jnp.concatenate([left_ops, right_ops], 0), "sector", partner)
    left_p, right_p = ops_p[:slots], ops_p[slots:]
    ints_p = lax.ppermute(jnp.concatenate([deltas, counts]), "sector", partner)
    deltas_p, counts_p = ints_p[:slots], ints_p[slots:]
    own_job = (left_ops, right_ops, deltas, counts)
    partner_job = (left_p, right_p, deltas_p, counts_p)

    partner_sum, own_sum = apply_pairs(0, (own, from_partner), ((False, partner_job), (True, own_job)), half)
    own_sum, partner_sum, from_far = lax.optimization_barrier((own_sum, partner_sum, from_far))
    (partner_half,) = apply_pairs(2, (from_far,), ((False, partner_job),), half, (partner_sum,))
    own_sum, partner_half, from_near = lax.optimization_barrier((own_sum, partner_half, from_near))
    returned = lax.ppermute(partner_half.reshape((half,) + own.shape[1:]), "sector", partner)
    (out,) = apply_pairs(1, (from_near,), ((True, own_job),), half, (own_sum,))
    out = jnp.concatenate([out.reshape((half,) + own.shape[1:]), returned], 0)
    return out[None]


def solution(mesh):
    return jax.shard_map(
        on_device,
        mesh=mesh,
        in_specs=(
            P(("group", "sector"), None, None, None),
            P(("group", "sector"), None, None),
            P(("group", "sector"), None, None),
            P(("group", "sector")),
            P(("group", "sector")),
        ),
        out_specs=P(("group", "sector"), None, None, None),
        check_vma=False,
    )
```

```python
import functools

import jax
import jax.numpy as jnp
from jax import lax
from jax.experimental import pallas as pl
from jax.experimental.pallas import tpu as pltpu
from jax.sharding import PartitionSpec as P


def source_of(delta, parity, own_job, phase):
    d = jnp.clip(delta, -1, 1)
    outer = 2 * parity - 1
    if own_job:
        if phase == 0:
            return jnp.where(d == 0, 0, jnp.where(d == -outer, 1, 2))
        return jnp.where(d == outer, 0, 2)
    if phase == 0:
        return jnp.where(d == 0, 1, jnp.where(d == outer, 0, 2))
    return jnp.where(d == -outer, 0, 2)


def pairs_kernel(phase, jobs, n_src, half, *refs):
    njobs = len(jobs)
    ints = refs[:2 * njobs]
    srcs = refs[2 * njobs:2 * njobs + n_src]
    ops = refs[2 * njobs + n_src:4 * njobs + n_src]
    rest = refs[4 * njobs + n_src:]
    starts = rest[:njobs] if phase > 0 else (None,) * njobs
    rest = rest[njobs:] if phase > 0 else rest
    outs, (acc_ref, mixed_ref) = rest[:njobs], rest[njobs:]
    width = srcs[0].shape[1]
    parity = lax.axis_index("sector") % 2
    for j, own_job in enumerate(jobs):
        deltas_ref, count_ref = ints[2 * j], ints[2 * j + 1]
        left_ref, right_ref = ops[2 * j], ops[2 * j + 1]
        start_ref, out_ref = starts[j], outs[j]
        first = 0 if (phase > 0 or own_job) else half
        if start_ref is None:
            acc_ref[...] = jnp.zeros_like(acc_ref)
        else:
            acc_ref[...] = start_ref[...]

        def step(k, carry, deltas_ref=deltas_ref, left_ref=left_ref, right_ref=right_ref, own_job=own_job, first=first):
            which = source_of(deltas_ref[k], parity, own_job, phase)

            @pl.when(which < n_src)
            def _():
                left = left_ref[k]

                def run(src_ref):
                    for r in range(half):
                        mixed_ref[pl.ds(r * width, width), :] = jnp.dot(
                            left, src_ref[first + r], preferred_element_type=jnp.float32
                        ).astype(jnp.bfloat16)

                for m, ref in enumerate(srcs):
                    pl.when(which == m)(functools.partial(run, ref))
                acc_ref[...] += lax.dot_general(
                    mixed_ref[...], right_ref[k], (((1,), (1,)), ((), ())), preferred_element_type=jnp.float32
                )

            return carry

        lax.fori_loop(0, jnp.minimum(count_ref[0], left_ref.shape[0]), step, 0)
        if phase > 0 and own_job:
            out_ref[pl.ds(0, half * width), :] = acc_ref[...].astype(out_ref.dtype)
        else:
            out_ref[...] = acc_ref[...].astype(out_ref.dtype)


def apply_pairs(phase, sources, jobs, half, starts=()):
    width = sources[0].shape[1]
    size = half * width
    slots = jobs[0][1][0].shape[0]
    vmem = pl.BlockSpec(memory_space=pltpu.VMEM)
    smem = pl.BlockSpec(memory_space=pltpu.SMEM)
    flops = 2 * slots * size * width * width * len(jobs) // 3
    moved = 2 * (len(sources) * size * width + 2 * len(jobs) * slots * width * width) + 8 * len(jobs) * size * width
    outs = []
    for is_own, _ in jobs:
        if phase == 0:
            outs.append(jax.ShapeDtypeStruct((size, width), jnp.float32))
        else:
            outs.append(jax.ShapeDtypeStruct(((2 if is_own else 1) * size, width), jnp.bfloat16))
    ints = [x for _, (l, r, d, c) in jobs for x in (d, c)]
    ops = [x for _, (l, r, d, c) in jobs for x in (l, r)]
    return pl.pallas_call(
        functools.partial(pairs_kernel, phase, tuple(o for o, _ in jobs), len(sources), half),
        out_shape=tuple(outs),
        in_specs=[smem] * len(ints) + [vmem] * (len(sources) + len(ops) + len(starts)),
        out_specs=tuple(vmem for _ in outs),
        scratch_shapes=[
            pltpu.VMEM((size, width), jnp.float32),
            pltpu.VMEM((size, width), jnp.bfloat16),
        ],
        cost_estimate=pl.CostEstimate(flops=flops, bytes_accessed=moved, transcendentals=0),
        compiler_params=pltpu.CompilerParams(vmem_limit_bytes=24 * 1024 * 1024),
    )(*ints, *sources, *ops, *starts)


def on_device(wave, left_ops, right_ops, deltas, counts):
    n = lax.axis_size("sector")
    own = wave[0]
    half = own.shape[0] // 2

    odd, even = range(1, n, 2), range(0, n, 2)
    near = [(j, j + 1) for j in odd if j + 1 < n] + [(j, j - 1) for j in even if j >= 2]
    far = [(j, j + 2) for j in odd if j + 2 < n] + [(j, j - 2) for j in even if j >= 2]
    partner = [(j, j ^ 1) for j in range(n)]

    from_near = lax.ppermute(own[:half], "sector", near)
    from_far = lax.ppermute(own[half:], "sector", far)
    from_partner = lax.ppermute(own, "sector", partner)

    slots = left_ops.shape[0]
    ops_p = lax.ppermute(jnp.concatenate([left_ops, right_ops], 0), "sector", partner)
    left_p, right_p = ops_p[:slots], ops_p[slots:]
    ints_p = lax.ppermute(jnp.concatenate([deltas, counts]), "sector", partner)
    deltas_p, counts_p = ints_p[:slots], ints_p[slots:]
    own_job = (left_ops, right_ops, deltas, counts)
    partner_job = (left_p, right_p, deltas_p, counts_p)

    partner_sum, own_sum = apply_pairs(0, (own, from_partner), ((False, partner_job), (True, own_job)), half)
    own_sum, partner_sum, from_far = lax.optimization_barrier((own_sum, partner_sum, from_far))
    (partner_half,) = apply_pairs(2, (from_far,), ((False, partner_job),), half, (partner_sum,))
    own_sum, partner_half, from_near = lax.optimization_barrier((own_sum, partner_half, from_near))
    returned = lax.ppermute(partner_half.reshape((half,) + own.shape[1:]), "sector", partner)
    (out,) = apply_pairs(1, (from_near,), ((True, own_job),), half, (own_sum,))
    out = lax.dynamic_update_slice_in_dim(out.reshape(own.shape), returned, half, 0)
    return out[None]


def solution(mesh):
    return jax.shard_map(
        on_device,
        mesh=mesh,
        in_specs=(
            P(("group", "sector"), None, None, None),
            P(("group", "sector"), None, None),
            P(("group", "sector"), None, None),
            P(("group", "sector")),
            P(("group", "sector")),
        ),
        out_specs=P(("group", "sector"), None, None, None),
        check_vma=False,
    )
```

```python
import functools

import jax
import jax.numpy as jnp
from jax import lax
from jax.experimental import pallas as pl
from jax.experimental.pallas import tpu as pltpu
from jax.sharding import PartitionSpec as P


def source_of(delta, parity, own_job, phase):
    d = jnp.clip(delta, -1, 1)
    outer = 2 * parity - 1
    if own_job:
        if phase == 0:
            return jnp.where(d == 0, 0, jnp.where(d == -outer, 1, 2))
        return jnp.where(d == outer, 0, 2)
    if phase == 0:
        return jnp.where(d == 0, 1, jnp.where(d == outer, 0, 2))
    return jnp.where(d == -outer, 0, 2)


def pairs_kernel(phase, jobs, n_src, half, *refs):
    njobs = len(jobs)
    ints = refs[:2 * njobs]
    srcs = refs[2 * njobs:2 * njobs + n_src]
    ops = refs[2 * njobs + n_src:4 * njobs + n_src]
    rest = refs[4 * njobs + n_src:]
    starts = rest[:njobs] if phase > 0 else (None,) * njobs
    rest = rest[njobs:] if phase > 0 else rest
    outs, (acc_ref, mixed_ref) = rest[:njobs], rest[njobs:]
    width = srcs[0].shape[1]
    parity = lax.axis_index("sector") % 2
    for j, own_job in enumerate(jobs):
        deltas_ref, count_ref = ints[2 * j], ints[2 * j + 1]
        left_ref, right_ref = ops[2 * j], ops[2 * j + 1]
        start_ref, out_ref = starts[j], outs[j]
        first = 0 if (phase > 0 or own_job) else half
        if start_ref is None:
            acc_ref[...] = jnp.zeros_like(acc_ref)
        else:
            acc_ref[...] = start_ref[...]

        def step(k, carry, deltas_ref=deltas_ref, left_ref=left_ref, right_ref=right_ref, own_job=own_job, first=first):
            which = source_of(deltas_ref[k], parity, own_job, phase)

            @pl.when(which < n_src)
            def _():
                left = left_ref[k]

                def run(src_ref):
                    for r in range(half):
                        mixed_ref[pl.ds(r * width, width), :] = jnp.dot(
                            left, src_ref[first + r], preferred_element_type=jnp.float32
                        ).astype(jnp.bfloat16)

                for m, ref in enumerate(srcs):
                    pl.when(which == m)(functools.partial(run, ref))
                acc_ref[...] += lax.dot_general(
                    mixed_ref[...], right_ref[k], (((1,), (1,)), ((), ())), preferred_element_type=jnp.float32
                )

            return carry

        lax.fori_loop(0, jnp.minimum(count_ref[0], left_ref.shape[0]), step, 0)
        if phase > 0 and own_job:
            out_ref[pl.ds(0, half * width), :] = acc_ref[...].astype(out_ref.dtype)
        else:
            out_ref[...] = acc_ref[...].astype(out_ref.dtype)


def apply_pairs(phase, sources, jobs, half, starts=()):
    width = sources[0].shape[1]
    size = half * width
    slots = jobs[0][1][0].shape[0]
    vmem = pl.BlockSpec(memory_space=pltpu.VMEM)
    smem = pl.BlockSpec(memory_space=pltpu.SMEM)
    flops = 2 * slots * size * width * width * len(jobs) // 3
    moved = 2 * (len(sources) * size * width + 2 * len(jobs) * slots * width * width) + 8 * len(jobs) * size * width
    outs = []
    for is_own, _ in jobs:
        if phase == 0:
            outs.append(jax.ShapeDtypeStruct((size, width), jnp.float32))
        else:
            outs.append(jax.ShapeDtypeStruct(((2 if is_own else 1) * size, width), jnp.bfloat16))
    ints = [x for _, (l, r, d, c) in jobs for x in (d, c)]
    ops = [x for _, (l, r, d, c) in jobs for x in (l, r)]
    return pl.pallas_call(
        functools.partial(pairs_kernel, phase, tuple(o for o, _ in jobs), len(sources), half),
        out_shape=tuple(outs),
        in_specs=[smem] * len(ints) + [vmem] * (len(sources) + len(ops) + len(starts)),
        out_specs=tuple(vmem for _ in outs),
        scratch_shapes=[
            pltpu.VMEM((size, width), jnp.float32),
            pltpu.VMEM((size, width), jnp.bfloat16),
        ],
        cost_estimate=pl.CostEstimate(flops=flops, bytes_accessed=moved, transcendentals=0),
        compiler_params=pltpu.CompilerParams(vmem_limit_bytes=24 * 1024 * 1024),
    )(*ints, *sources, *ops, *starts)


def on_device(wave, left_ops, right_ops, deltas, counts):
    n = lax.axis_size("sector")
    own = wave[0]
    half = own.shape[0] // 2

    odd, even = range(1, n, 2), range(0, n, 2)
    near = [(j, j + 1) for j in odd if j + 1 < n] + [(j, j - 1) for j in even if j >= 2]
    far = [(j, j + 2) for j in odd if j + 2 < n] + [(j, j - 2) for j in even if j >= 2]
    partner = [(j, j ^ 1) for j in range(n)]

    from_near = lax.ppermute(own[:half], "sector", near)
    from_far = lax.ppermute(own[half:], "sector", far)
    from_partner = lax.ppermute(own, "sector", partner)

    slots = left_ops.shape[0]
    ops_p = lax.ppermute(jnp.concatenate([left_ops, right_ops], 0), "sector", partner)
    left_p, right_p = ops_p[:slots], ops_p[slots:]
    ints_p = lax.ppermute(jnp.concatenate([deltas, counts]), "sector", partner)
    deltas_p, counts_p = ints_p[:slots], ints_p[slots:]
    own_job = (left_ops, right_ops, deltas, counts)
    partner_job = (left_p, right_p, deltas_p, counts_p)

    partner_sum, own_sum = apply_pairs(0, (own, from_partner), ((False, partner_job), (True, own_job)), half)
    own_sum, partner_sum, from_far = lax.optimization_barrier((own_sum, partner_sum, from_far))
    (partner_half,) = apply_pairs(2, (from_far,), ((False, partner_job),), half, (partner_sum,))
    returned = lax.ppermute(partner_half.reshape((half,) + own.shape[1:]), "sector", partner)
    own_sum, partner_half, from_near = lax.optimization_barrier((own_sum, partner_half, from_near))
    (out,) = apply_pairs(1, (from_near,), ((True, own_job),), half, (own_sum,))
    out = lax.dynamic_update_slice_in_dim(out.reshape(own.shape), returned, half, 0)
    return out[None]


def solution(mesh):
    return jax.shard_map(
        on_device,
        mesh=mesh,
        in_specs=(
            P(("group", "sector"), None, None, None),
            P(("group", "sector"), None, None),
            P(("group", "sector"), None, None),
            P(("group", "sector")),
            P(("group", "sector")),
        ),
        out_specs=P(("group", "sector"), None, None, None),
        check_vma=False,
    )
```
